768 devices in a mesh: dp: 2 (over z_hi), ctx: 96 (over z_lo, y, core), fsdp: 4 (over x).
Axes of the slice: x: 4, y: 8, z: 12 (z_hi: 2, z_lo: 6; z = z_hi * 6 + z_lo), core: 2. Of those that a mesh axis runs over, the one named last changes fastest.
Arguments:
- query: bfloat16 [2, 49152, 2048], P('dp', 'ctx', 'fsdp'), may hold values from -6 to 6
- key: bfloat16 [2, 49152, 1024], P('dp', 'ctx', 'fsdp'), may hold values from -6 to 6
- value: bfloat16 [2, 49152, 1024], P('dp', 'ctx', 'fsdp'), may hold values from -6 to 6
- out_grad: bfloat16 [2, 49152, 2048], P('dp', 'ctx', 'fsdp'), may hold values from -48 to 48
- query_gain: float32 [128], replicated, may hold values from 0.25 to 1.75
- key_gain: float32 [128], replicated, may hold values from 0.25 to 1.75
- list_start: int32 [2, 49152], P('dp', 'ctx'), may hold values from 0 to 49151, as said below
Outputs:
- query_grad: bfloat16 [2, 49152, 2048], P('dp', 'ctx', 'fsdp')
- key_grad: bfloat16 [2, 49152, 1024], P('dp', 'ctx', 'fsdp')
- value_grad: bfloat16 [2, 49152, 1024], P('dp', 'ctx', 'fsdp')
- gain_grads: float32 [2, 128], replicated
The draws below stay inside these ranges and needn't reach their ends.
Inputs may be any that keep to these rules, and one draw needn't show every extreme that they name: list_start of a token is at most its own position and never falls along a sequence; it equals the position where a new candidate list begins; positions 0 and 49151 each begin a list.
All inputs are finite; a program needn't handle non-finite values.
Results may differ from the reference program's by a relative error of at most 0.0078.
Values may be sent and summed in bfloat16 or wider, within the bound.
No kernel may reach another device: no remote copies, remote signals or barrier semaphores. Data moves between devices by JAX's collectives and lax.ppermute only.
A program may use at most 64 MiB of HBM per device.

```python
import jax
import jax.numpy as jnp
from jax import lax

HD = 128
HQ = 16
HK = 8
WINDOW = 1024
QSCALAR = 168
TOK_DEV = 512
LENGTH = 49152
SEQS = 2


def draw_list_start(key, part):
    places = jnp.broadcast_to(jnp.arange(LENGTH, dtype=jnp.int32), (SEQS, LENGTH))
    boundary = jax.random.randint(key, (SEQS, LENGTH), 0, 2 * WINDOW // 3 + 1) == 0
    boundary = boundary | (places == 0) | (places == LENGTH - 1)
    return lax.cummax(jnp.where(boundary, places, 0), axis=1).astype(jnp.int32)


def levels(stream_key, dims, cuts, smallest, largest):
    factor_of = 1.0
    for position, shards_of in cuts:
        steps = jax.random.uniform(jax.random.fold_in(jax.random.fold_in(stream_key, 6), position), (shards_of,), jnp.float32, smallest / len(cuts), largest / len(cuts))
        factor_of = factor_of * jnp.repeat(jnp.exp(steps), dims[position] // shards_of).reshape((-1,) + (1,) * (len(dims) - 1 - position))
    return factor_of


def normal_values(rng, dims, deviation, most, pieces=(), kind=jnp.bfloat16):
    entries = deviation * jax.random.normal(rng, dims, jnp.float32)
    if pieces:
        entries = entries * levels(rng, dims, pieces, -0.22, 0.18)
    return jnp.clip(entries, -most, most).astype(kind)


def setup_inputs(seed: int = 0) -> dict:
    seeds = jax.random.split(jax.random.key(seed), 8)
    return {
        "query": normal_values(seeds[0], (SEQS, LENGTH, HQ * HD), 1.0, 6.0, ((0, 2), (1, 96), (2, 4))),
        "key": normal_values(seeds[1], (SEQS, LENGTH, HK * HD), 1.0, 6.0, ((0, 2), (1, 96), (2, 4))),
        "value": normal_values(seeds[2], (SEQS, LENGTH, HK * HD), 1.0, 6.0, ((0, 2), (1, 96), (2, 4))),
        "out_grad": normal_values(seeds[3], (SEQS, LENGTH, HQ * HD), 8.0, 48.0, ((0, 2), (1, 96), (2, 4))),
        "query_gain": jnp.clip(1.0 + 0.15 * jax.random.normal(seeds[4], (HD,), jnp.float32), 0.25, 1.75),
        "key_gain": jnp.clip(1.0 + 0.15 * jax.random.normal(seeds[5], (HD,), jnp.float32), 0.25, 1.75),
        "list_start": draw_list_start(jax.random.fold_in(seeds[7], 71), 0),
    }


epsilon = 1e-06

def normalize(raw, gain, factor):
    values = raw.astype(jnp.float32)
    inverse = lax.rsqrt(lax.optimization_barrier(jnp.mean(values * values, axis=-1, keepdims=True)) + epsilon)
    unit_rows = values * inverse
    return (unit_rows, inverse, (unit_rows * gain * factor).astype(jnp.bfloat16))

def norm_backward(grad_n, unit_rows, inverse, gain, factor):
    grad_hat = grad_n * gain * factor
    return (grad_hat - unit_rows * lax.optimization_barrier(jnp.mean(grad_hat * unit_rows, axis=-1, keepdims=True))) * inverse

def one_sequence(query, key, value, out_grad, query_gain, key_gain, list_start):
    group_size = HQ // HK
    factor = QSCALAR ** (-0.5)
    query_hat, query_inv, query_n = normalize(query.reshape(LENGTH, HK, group_size, HD), query_gain, factor)
    key_hat, key_inv, key_n = normalize(key.reshape(LENGTH, HK, HD), key_gain, 1.0)
    values = value.reshape(LENGTH, HK, HD)
    grads_in = out_grad.reshape(LENGTH, HK, group_size, HD)
    block = TOK_DEV
    span = WINDOW + block
    padded_keys = jnp.concatenate([jnp.zeros((WINDOW, HK, HD), jnp.bfloat16), key_n], axis=0)
    padded_values = jnp.concatenate([jnp.zeros((WINDOW, HK, HD), jnp.bfloat16), values], axis=0)
    highest = lax.Precision.HIGHEST

    def step(pending, index):
        key_acc, value_acc = pending
        first = index * block
        query_block = lax.dynamic_slice_in_dim(query_n, first, block, 0).astype(jnp.float32)
        grad_block = lax.dynamic_slice_in_dim(grads_in, first, block, 0).astype(jnp.float32)
        key_block = lax.dynamic_slice_in_dim(padded_keys, first, span, 0).astype(jnp.float32)
        value_block = lax.dynamic_slice_in_dim(padded_values, first, span, 0).astype(jnp.float32)
        starts = lax.dynamic_slice_in_dim(list_start, first, block, 0)
        query_place = first + jnp.arange(block, dtype=jnp.int32)
        key_place = first - WINDOW + jnp.arange(span, dtype=jnp.int32)
        allowed = (key_place[None, :] >= starts[:, None]) & (key_place[None, :] <= query_place[:, None]) & (query_place[:, None] - key_place[None, :] < WINDOW)
        scores = jnp.einsum('tkgd,ukd->kgtu', query_block, key_block, precision=highest)
        weight = jnp.where(allowed, jnp.exp(scores), 0.0)
        denominator = lax.optimization_barrier(jnp.sum(weight, axis=-1, keepdims=True))
        prob = lax.optimization_barrier((weight / denominator).astype(jnp.bfloat16)).astype(jnp.float32)
        attended = jnp.einsum('kgtu,ukd->tkgd', prob, value_block, precision=highest)
        row_term = jnp.transpose(lax.optimization_barrier(jnp.sum(grad_block * attended, axis=-1)), (1, 2, 0))[..., None]
        products = jnp.einsum('tkgd,ukd->kgtu', grad_block, value_block, precision=highest)
        dscore = lax.optimization_barrier((prob * (products - row_term)).astype(jnp.bfloat16)).astype(jnp.float32)
        dquery_part = jnp.einsum('kgtu,ukd->tkgd', dscore, key_block, precision=highest)
        dkey_part = jnp.einsum('kgtu,tkgd->ukd', dscore, query_block, precision=highest)
        dvalue_part = jnp.einsum('kgtu,tkgd->ukd', prob, grad_block, precision=highest)
        key_acc = lax.dynamic_update_slice_in_dim(key_acc, lax.dynamic_slice_in_dim(key_acc, first, span, 0) + dkey_part, first, 0)
        value_acc = lax.dynamic_update_slice_in_dim(value_acc, lax.dynamic_slice_in_dim(value_acc, first, span, 0) + dvalue_part, first, 0)
        return ((key_acc, value_acc), dquery_part)
    empty = jnp.zeros((LENGTH + WINDOW, HK, HD), jnp.float32)
    (key_acc, value_acc), dquery_blocks = lax.scan(step, (empty, empty), jnp.arange(LENGTH // block, dtype=jnp.int32))
    dquery_n = dquery_blocks.reshape(LENGTH, HK, group_size, HD)
    dkey_n = key_acc[WINDOW:]
    query_grad = norm_backward(dquery_n, query_hat, query_inv, query_gain, factor).astype(jnp.bfloat16).reshape(LENGTH, HQ * HD)
    key_grad = norm_backward(dkey_n, key_hat, key_inv, key_gain, 1.0).astype(jnp.bfloat16).reshape(LENGTH, HK * HD)
    value_grad = value_acc[WINDOW:].astype(jnp.bfloat16).reshape(LENGTH, HK * HD)
    query_term = lax.optimization_barrier(jnp.sum(dquery_n * query_hat, axis=(0, 1, 2))) * factor
    key_term = lax.optimization_barrier(jnp.sum(dkey_n * key_hat, axis=(0, 1)))
    return (query_grad, key_grad, value_grad, query_term, key_term)

def reference(query, key, value, out_grad, query_gain, key_gain, list_start):
    results = [one_sequence(query[row], key[row], value[row], out_grad[row], query_gain, key_gain, list_start[row]) for row in range(SEQS)]
    query_grad = jnp.stack([item[0] for item in results])
    key_grad = jnp.stack([item[1] for item in results])
    value_grad = jnp.stack([item[2] for item in results])
    query_total = results[0][3]
    key_total = results[0][4]
    for item in results[1:]:
        query_total = query_total + item[3]
        key_total = key_total + item[4]
    gain_grads = jnp.stack([query_total * (SEQS * LENGTH * HQ) ** (-0.5), key_total * (SEQS * LENGTH * HK) ** (-0.5)]).astype(jnp.float32)
    return (query_grad, key_grad, value_grad, gain_grads)
```

```python
import jax
import jax.numpy as jnp
from jax import lax
from jax.sharding import PartitionSpec as P

HD = 128
HQ = 16
HK = 8
WINDOW = 1024
QSCALAR = 168


epsilon = 1e-06


def passed_along(value, axis, steps):
    count = lax.axis_size(axis)
    initial, last = (max(0, -steps), min(count, count - steps))
    return lax.ppermute(value, axis, [(source, source + steps) for source in range(initial, last)])


def exchanged_sum(value, axis, stride):
    count = lax.axis_size(axis)
    return value + lax.ppermute(value, axis, [(source, source ^ stride) for source in range(count)])


def three_way_sum(value, axis, stride):
    count = lax.axis_size(axis)
    digit = (lax.axis_index(axis) // stride) % 3
    received = [value]
    for shift in (1, 2):
        pairs = []
        for source in range(count):
            place = (source // stride) % 3
            pairs.append((source, source + ((place + shift) % 3 - place) * stride))
        received.append(lax.ppermute(value, axis, pairs))
    ordered = []
    for place in range(3):
        pick = received[0]
        for shift in (1, 2):
            pick = jnp.where((digit - shift) % 3 == place, received[shift], pick)
        pick = jnp.where(digit == place, received[0], pick)
        ordered.append(pick)
    return ordered[0] + ordered[1] + ordered[2]


def total_over_devices(value):
    value = exchanged_sum(value, "fsdp", 1)
    value = exchanged_sum(value, "fsdp", 2)
    value = exchanged_sum(value, "dp", 1)
    for stride in (1, 2, 4, 8, 16):
        value = exchanged_sum(value, "ctx", stride)
    return three_way_sum(value, "ctx", 32)


def normalize(raw, gain, factor):
    values = raw.astype(jnp.float32)
    inverse = lax.rsqrt(jnp.mean(values * values, axis=-1, keepdims=True) + epsilon)
    unit_rows = values * inverse
    return (unit_rows, inverse, (unit_rows * gain * factor).astype(jnp.bfloat16))


def norm_backward(grad_n, unit_rows, inverse, gain, factor):
    grad_hat = grad_n * gain * factor
    return (grad_hat - unit_rows * jnp.mean(grad_hat * unit_rows, axis=-1, keepdims=True)) * inverse


def shards(query, key, value, out_grad, query_gain, key_gain, list_start):
    tokens = query.shape[1]
    kv_heads = key.shape[2] // HD
    group_size = query.shape[2] // key.shape[2]
    factor = QSCALAR ** (-0.5)
    reach = WINDOW // tokens
    query_hat, query_inv, query_n = normalize(
        query[0].reshape(tokens, kv_heads, group_size, HD), query_gain, factor
    )
    key_hat, key_inv, key_n = normalize(key[0].reshape(tokens, kv_heads, HD), key_gain, 1.0)
    own_values = value[0].reshape(tokens, kv_heads, HD)
    grads_in = out_grad[0].reshape(tokens, kv_heads, group_size, HD)
    starts = list_start[0]
    anchor = lax.axis_index("ctx") * tokens
    query_place = anchor + jnp.arange(tokens, dtype=jnp.int32)
    blocks = [(key_n, own_values)]
    for distance in range(1, reach + 1):
        blocks.append(passed_along((key_n, own_values), "ctx", distance))
    allowed_sets = []
    for distance in range(reach + 1):
        key_place = anchor - distance * tokens + jnp.arange(tokens, dtype=jnp.int32)
        allowed_sets.append(
            (key_place[None, :] >= starts[:, None])
            & (key_place[None, :] <= query_place[:, None])
            & (query_place[:, None] - key_place[None, :] < WINDOW)
        )

    def forward_block(operands):
        allowed, key_block = operands
        scores = jnp.einsum(
            "tkgd,ukd->kgtu", query_n, key_block, preferred_element_type=jnp.float32
        )
        return jnp.where(allowed[None, None], jnp.exp(scores), 0.0)

    cached = [forward_block((allowed_sets[index], blocks[index][0])) for index in range(reach + 1)]
    denominator = jnp.sum(cached[0], axis=-1, keepdims=True)
    for weight in cached[1:]:
        denominator = denominator + jnp.sum(weight, axis=-1, keepdims=True)
    weights_bf = [(weight / denominator).astype(jnp.bfloat16) for weight in cached]
    attend_zero = jnp.zeros((tokens, kv_heads, group_size, HD), jnp.float32)
    attended = attend_zero
    for index in range(reach + 1):
        attend_prob = weights_bf[index]
        attend_value_block = blocks[index][1]
        attended = attended + jnp.einsum(
            "kgtu,ukd->tkgd", attend_prob, attend_value_block, preferred_element_type=jnp.float32
        )
    row_term = jnp.transpose(jnp.sum(grads_in.astype(jnp.float32) * attended, axis=-1), (1, 2, 0))[
        ..., None
    ]
    dquery_n = attend_zero
    pieces = []
    for index in range(reach + 1):
        prob = weights_bf[index]
        backward_key_block = blocks[index][0]
        value_block = blocks[index][1]
        products = jnp.einsum(
            "tkgd,ukd->kgtu", grads_in, value_block, preferred_element_type=jnp.float32
        )
        dscore = (prob.astype(jnp.float32) * (products - row_term)).astype(jnp.bfloat16)
        dquery_part = jnp.einsum(
            "kgtu,ukd->tkgd", dscore, backward_key_block, preferred_element_type=jnp.float32
        )
        dkey_part = jnp.einsum(
            "kgtu,tkgd->ukd", dscore, query_n, preferred_element_type=jnp.float32
        )
        dvalue_part = jnp.einsum(
            "kgtu,tkgd->ukd", prob, grads_in, preferred_element_type=jnp.float32
        )
        dquery_n = dquery_n + dquery_part
        pieces.append((dkey_part, dvalue_part))
    dkey_n = pieces[0][0]
    dvalue_sum = pieces[0][1]
    for distance in range(1, reach + 1):
        returned = passed_along(pieces[distance], "ctx", -distance)
        dkey_n = dkey_n + returned[0]
        dvalue_sum = dvalue_sum + returned[1]
    query_grad = (
        norm_backward(dquery_n, query_hat, query_inv, query_gain, factor)
        .astype(jnp.bfloat16)
        .reshape(1, tokens, -1)
    )
    key_grad = (
        norm_backward(dkey_n, key_hat, key_inv, key_gain, 1.0)
        .astype(jnp.bfloat16)
        .reshape(1, tokens, -1)
    )
    value_grad = dvalue_sum.astype(jnp.bfloat16).reshape(1, tokens, -1)
    partial_sums = jnp.stack(
        [
            jnp.sum(dquery_n * query_hat, axis=(0, 1, 2)) * factor,
            jnp.sum(dkey_n * key_hat, axis=(0, 1)),
        ]
    )
    summed = total_over_devices(partial_sums)
    counted = lax.axis_size("dp") * lax.axis_size("ctx") * tokens
    normalizers = jnp.array([[(counted * HQ) ** (-0.5)], [(counted * HK) ** (-0.5)]], jnp.float32)
    return (query_grad, key_grad, value_grad, summed * normalizers)


def solution(mesh):
    in_specs = (
        P("dp", "ctx", "fsdp"),
        P("dp", "ctx", "fsdp"),
        P("dp", "ctx", "fsdp"),
        P("dp", "ctx", "fsdp"),
        P(),
        P(),
        P("dp", "ctx"),
    )
    out_specs = (P("dp", "ctx", "fsdp"), P("dp", "ctx", "fsdp"), P("dp", "ctx", "fsdp"), P())
    return jax.shard_map(shards, mesh=mesh, in_specs=in_specs, out_specs=out_specs, check_vma=False)
```

```python
import jax
import jax.numpy as jnp
from jax import lax
from jax.sharding import PartitionSpec as P

HD = 128
HQ = 16
HK = 8
WINDOW = 1024
QSCALAR = 168


epsilon = 1e-06


def passed_along(value, axis, steps):
    count = lax.axis_size(axis)
    initial, last = (max(0, -steps), min(count, count - steps))
    return lax.ppermute(value, axis, [(source, source + steps) for source in range(initial, last)])


def exchanged_sum(value, axis, stride):
    count = lax.axis_size(axis)
    return value + lax.ppermute(value, axis, [(source, source ^ stride) for source in range(count)])


def three_way_sum(value, axis, stride):
    count = lax.axis_size(axis)
    digit = (lax.axis_index(axis) // stride) % 3
    received = [value]
    for shift in (1, 2):
        pairs = []
        for source in range(count):
            place = (source // stride) % 3
            pairs.append((source, source + ((place + shift) % 3 - place) * stride))
        received.append(lax.ppermute(value, axis, pairs))
    ordered = []
    for place in range(3):
        pick = received[0]
        for shift in (1, 2):
            pick = jnp.where((digit - shift) % 3 == place, received[shift], pick)
        pick = jnp.where(digit == place, received[0], pick)
        ordered.append(pick)
    return ordered[0] + ordered[1] + ordered[2]


def total_over_devices(value):
    value = exchanged_sum(value, "fsdp", 1)
    value = exchanged_sum(value, "fsdp", 2)
    value = exchanged_sum(value, "dp", 1)
    for stride in (1, 2, 4, 8, 16):
        value = exchanged_sum(value, "ctx", stride)
    return three_way_sum(value, "ctx", 32)


def normalize(raw, gain, factor):
    values = raw.astype(jnp.float32)
    inverse = lax.rsqrt(jnp.mean(values * values, axis=-1, keepdims=True) + epsilon)
    unit_rows = values * inverse
    return (unit_rows, inverse, (unit_rows * gain * factor).astype(jnp.bfloat16))


def norm_backward(grad_n, unit_rows, inverse, gain, factor):
    grad_hat = grad_n * gain * factor
    return (grad_hat - unit_rows * jnp.mean(grad_hat * unit_rows, axis=-1, keepdims=True)) * inverse


def shards(query, key, value, out_grad, query_gain, key_gain, list_start):
    tokens = query.shape[1]
    kv_heads = key.shape[2] // HD
    group_size = query.shape[2] // key.shape[2]
    factor = QSCALAR ** (-0.5)
    reach = WINDOW // tokens
    query_hat, query_inv, query_n = normalize(
        query[0].reshape(tokens, kv_heads, group_size, HD), query_gain, factor
    )
    key_raw = key[0].reshape(tokens, kv_heads, HD)
    key_hat, key_inv, key_n = normalize(key_raw, key_gain, 1.0)
    own_values = value[0].reshape(tokens, kv_heads, HD)
    grads_in = out_grad[0].reshape(tokens, kv_heads, group_size, HD)
    starts = list_start[0]
    anchor = lax.axis_index("ctx") * tokens
    query_place = anchor + jnp.arange(tokens, dtype=jnp.int32)
    packed = jnp.concatenate([key_raw, own_values], axis=-1)
    blocks = [(key_n, own_values)]
    block_hats = [key_hat]
    for distance in range(1, reach + 1):
        arrived = passed_along(packed, "ctx", distance)
        arrived_hat, _, arrived_n = normalize(arrived[..., :HD], key_gain, 1.0)
        blocks.append((arrived_n, arrived[..., HD:]))
        block_hats.append(arrived_hat)
    allowed_sets = []
    for distance in range(reach + 1):
        key_place = anchor - distance * tokens + jnp.arange(tokens, dtype=jnp.int32)
        allowed_sets.append(
            (key_place[None, :] >= starts[:, None])
            & (key_place[None, :] <= query_place[:, None])
            & (query_place[:, None] - key_place[None, :] < WINDOW)
        )

    def forward_block(operands):
        allowed, key_block = operands
        scores = jnp.einsum(
            "tkgd,ukd->kgtu", query_n, key_block, preferred_element_type=jnp.float32
        )
        return jnp.where(allowed[None, None], jnp.exp(scores), 0.0)

    cached = [forward_block((allowed_sets[index], blocks[index][0])) for index in range(reach + 1)]
    denominator = jnp.sum(cached[0], axis=-1, keepdims=True)
    for weight in cached[1:]:
        denominator = denominator + jnp.sum(weight, axis=-1, keepdims=True)
    weights_bf = [(weight / denominator).astype(jnp.bfloat16) for weight in cached]
    attend_zero = jnp.zeros((tokens, kv_heads, group_size, HD), jnp.float32)
    attended = attend_zero
    for index in range(reach + 1):
        attend_prob = weights_bf[index]
        attend_value_block = blocks[index][1]
        attended = attended + jnp.einsum(
            "kgtu,ukd->tkgd", attend_prob, attend_value_block, preferred_element_type=jnp.float32
        )
    row_term = jnp.transpose(jnp.sum(grads_in.astype(jnp.float32) * attended, axis=-1), (1, 2, 0))[
        ..., None
    ]
    dquery_n = attend_zero
    pieces = []
    for index in range(reach + 1):
        prob = weights_bf[index]
        backward_key_block = blocks[index][0]
        value_block = blocks[index][1]
        products = jnp.einsum(
            "tkgd,ukd->kgtu", grads_in, value_block, preferred_element_type=jnp.float32
        )
        dscore = (prob.astype(jnp.float32) * (products - row_term)).astype(jnp.bfloat16)
        dquery_part = jnp.einsum(
            "kgtu,ukd->tkgd", dscore, backward_key_block, preferred_element_type=jnp.float32
        )
        dkey_part = jnp.einsum(
            "kgtu,tkgd->ukd", dscore, query_n, preferred_element_type=jnp.float32
        )
        dvalue_part = jnp.einsum(
            "kgtu,tkgd->ukd", prob, grads_in, preferred_element_type=jnp.float32
        )
        dquery_n = dquery_n + dquery_part
        pieces.append((dkey_part, dvalue_part))
    key_term = jnp.sum(pieces[0][0] * block_hats[0], axis=(0, 1))
    for distance in range(1, reach + 1):
        key_term = key_term + jnp.sum(pieces[distance][0] * block_hats[distance], axis=(0, 1))
    partial_sums = jnp.stack([jnp.sum(dquery_n * query_hat, axis=(0, 1, 2)) * factor, key_term])
    summed = total_over_devices(partial_sums)
    dkey_n = pieces[0][0]
    dvalue_sum = pieces[0][1]
    for distance in range(1, reach + 1):
        returned = passed_along(jnp.concatenate(pieces[distance], axis=-1), "ctx", -distance)
        dkey_n = dkey_n + returned[..., :HD]
        dvalue_sum = dvalue_sum + returned[..., HD:]
    query_grad = (
        norm_backward(dquery_n, query_hat, query_inv, query_gain, factor)
        .astype(jnp.bfloat16)
        .reshape(1, tokens, -1)
    )
    key_grad = (
        norm_backward(dkey_n, key_hat, key_inv, key_gain, 1.0)
        .astype(jnp.bfloat16)
        .reshape(1, tokens, -1)
    )
    value_grad = dvalue_sum.astype(jnp.bfloat16).reshape(1, tokens, -1)
    counted = lax.axis_size("dp") * lax.axis_size("ctx") * tokens
    normalizers = jnp.array([[(counted * HQ) ** (-0.5)], [(counted * HK) ** (-0.5)]], jnp.float32)
    return (query_grad, key_grad, value_grad, summed * normalizers)


def solution(mesh):
    in_specs = (
        P("dp", "ctx", "fsdp"),
        P("dp", "ctx", "fsdp"),
        P("dp", "ctx", "fsdp"),
        P("dp", "ctx", "fsdp"),
        P(),
        P(),
        P("dp", "ctx"),
    )
    out_specs = (P("dp", "ctx", "fsdp"), P("dp", "ctx", "fsdp"), P("dp", "ctx", "fsdp"), P())
    return jax.shard_map(shards, mesh=mesh, in_specs=in_specs, out_specs=out_specs, check_vma=False)
```

```python
import jax
import jax.numpy as jnp
from jax import lax
from jax.sharding import PartitionSpec as P

HD = 128
HQ = 16
HK = 8
WINDOW = 1024
QSCALAR = 168


epsilon = 1e-06


def passed_along(value, axis, steps):
    count = lax.axis_size(axis)
    initial, last = (max(0, -steps), min(count, count - steps))
    return lax.ppermute(value, axis, [(source, source + steps) for source in range(initial, last)])


def exchanged_sum(value, axis, stride):
    count = lax.axis_size(axis)
    return value + lax.ppermute(value, axis, [(source, source ^ stride) for source in range(count)])


def three_way_sum(value, axis, stride):
    count = lax.axis_size(axis)
    digit = (lax.axis_index(axis) // stride) % 3
    received = [value]
    for shift in (1, 2):
        pairs = []
        for source in range(count):
            place = (source // stride) % 3
            pairs.append((source, source + ((place + shift) % 3 - place) * stride))
        received.append(lax.ppermute(value, axis, pairs))
    ordered = []
    for place in range(3):
        pick = received[0]
        for shift in (1, 2):
            pick = jnp.where((digit - shift) % 3 == place, received[shift], pick)
        pick = jnp.where(digit == place, received[0], pick)
        ordered.append(pick)
    return ordered[0] + ordered[1] + ordered[2]


def total_over_devices(value):
    value = exchanged_sum(value, "fsdp", 1)
    value = exchanged_sum(value, "fsdp", 2)
    value = exchanged_sum(value, "dp", 1)
    for stride in (1, 2, 4, 8, 16):
        value = exchanged_sum(value, "ctx", stride)
    return three_way_sum(value, "ctx", 32)


def normalize(raw, gain, factor):
    values = raw.astype(jnp.float32)
    inverse = lax.rsqrt(jnp.mean(values * values, axis=-1, keepdims=True) + epsilon)
    unit_rows = values * inverse
    return (unit_rows, inverse, (unit_rows * gain * factor).astype(jnp.bfloat16))


def norm_backward(grad_n, unit_rows, inverse, gain, factor):
    grad_hat = grad_n * gain * factor
    return (grad_hat - unit_rows * jnp.mean(grad_hat * unit_rows, axis=-1, keepdims=True)) * inverse


def shards(query, key, value, out_grad, query_gain, key_gain, list_start):
    tokens = query.shape[1]
    kv_heads = key.shape[2] // HD
    group_size = query.shape[2] // key.shape[2]
    factor = QSCALAR ** (-0.5)
    reach = WINDOW // tokens
    query_hat, query_inv, query_n = normalize(
        query[0].reshape(tokens, kv_heads, group_size, HD), query_gain, factor
    )
    key_raw = key[0].reshape(tokens, kv_heads, HD)
    key_hat, key_inv, key_n = normalize(key_raw, key_gain, 1.0)
    own_values = value[0].reshape(tokens, kv_heads, HD)
    grads_in = out_grad[0].reshape(tokens, kv_heads, group_size, HD)
    starts = list_start[0]
    anchor = lax.axis_index("ctx") * tokens
    query_place = anchor + jnp.arange(tokens, dtype=jnp.int32)
    packed = jnp.concatenate([key_raw, own_values], axis=-1)
    blocks = [(key_n, own_values)]
    block_hats = [key_hat]
    for distance in range(1, reach + 1):
        arrived = passed_along(packed, "ctx", distance)
        arrived_hat, _, arrived_n = normalize(arrived[..., :HD], key_gain, 1.0)
        blocks.append((arrived_n, arrived[..., HD:]))
        block_hats.append(arrived_hat)
    allowed_sets = []
    for distance in range(reach + 1):
        key_place = anchor - distance * tokens + jnp.arange(tokens, dtype=jnp.int32)
        allowed_sets.append(
            (key_place[None, :] >= starts[:, None])
            & (key_place[None, :] <= query_place[:, None])
            & (query_place[:, None] - key_place[None, :] < WINDOW)
        )

    def forward_block(operands):
        allowed, key_block = operands
        scores = jnp.einsum(
            "tkgd,ukd->kgtu", query_n, key_block, preferred_element_type=jnp.float32
        )
        return jnp.where(allowed[None, None], jnp.exp(scores), 0.0)

    cached = [forward_block((allowed_sets[index], blocks[index][0])) for index in range(reach + 1)]
    denominator = jnp.sum(cached[0], axis=-1, keepdims=True)
    for weight in cached[1:]:
        denominator = denominator + jnp.sum(weight, axis=-1, keepdims=True)
    weights_bf = [(weight / denominator).astype(jnp.bfloat16) for weight in cached]
    attend_zero = jnp.zeros((tokens, kv_heads, group_size, HD), jnp.float32)
    attended = attend_zero
    for index in range(reach + 1):
        attend_prob = weights_bf[index]
        attend_value_block = blocks[index][1]
        attended = attended + jnp.einsum(
            "kgtu,ukd->tkgd", attend_prob, attend_value_block, preferred_element_type=jnp.float32
        )
    row_term = jnp.transpose(jnp.sum(grads_in.astype(jnp.float32) * attended, axis=-1), (1, 2, 0))[
        ..., None
    ]
    dquery_n = attend_zero
    pieces = []
    for index in range(reach + 1):
        prob = weights_bf[index]
        backward_key_block = blocks[index][0]
        value_block = blocks[index][1]
        products = jnp.einsum(
            "tkgd,ukd->kgtu", grads_in, value_block, preferred_element_type=jnp.float32
        )
        dscore = (prob.astype(jnp.float32) * (products - row_term)).astype(jnp.bfloat16)
        dquery_part = jnp.einsum(
            "kgtu,ukd->tkgd", dscore, backward_key_block, preferred_element_type=jnp.float32
        )
        dkey_part = jnp.einsum(
            "kgtu,tkgd->ukd", dscore, query_n, preferred_element_type=jnp.float32
        )
        dvalue_part = jnp.einsum(
            "kgtu,tkgd->ukd", prob, grads_in, preferred_element_type=jnp.float32
        )
        dquery_n = dquery_n + dquery_part
        pieces.append((dkey_part, dvalue_part))
    key_term = jnp.sum(pieces[0][0] * block_hats[0], axis=(0, 1))
    for distance in range(1, reach + 1):
        key_term = key_term + jnp.sum(pieces[distance][0] * block_hats[distance], axis=(0, 1))
    partial_sums = jnp.stack([jnp.sum(dquery_n * query_hat, axis=(0, 1, 2)) * factor, key_term])
    summed = total_over_devices(partial_sums)
    returns = [
        passed_along(jnp.concatenate(pieces[distance], axis=-1), "ctx", -distance)
        for distance in range(1, reach + 1)
    ]
    summed, *returns = lax.optimization_barrier((summed, *returns))
    dkey_n = pieces[0][0]
    dvalue_sum = pieces[0][1]
    for returned in returns:
        dkey_n = dkey_n + returned[..., :HD]
        dvalue_sum = dvalue_sum + returned[..., HD:]
    query_grad = (
        norm_backward(dquery_n, query_hat, query_inv, query_gain, factor)
        .astype(jnp.bfloat16)
        .reshape(1, tokens, -1)
    )
    key_grad = (
        norm_backward(dkey_n, key_hat, key_inv, key_gain, 1.0)
        .astype(jnp.bfloat16)
        .reshape(1, tokens, -1)
    )
    value_grad = dvalue_sum.astype(jnp.bfloat16).reshape(1, tokens, -1)
    counted = lax.axis_size("dp") * lax.axis_size("ctx") * tokens
    normalizers = jnp.array([[(counted * HQ) ** (-0.5)], [(counted * HK) ** (-0.5)]], jnp.float32)
    return (query_grad, key_grad, value_grad, summed * normalizers)


def solution(mesh):
    in_specs = (
        P("dp", "ctx", "fsdp"),
        P("dp", "ctx", "fsdp"),
        P("dp", "ctx", "fsdp"),
        P("dp", "ctx", "fsdp"),
        P(),
        P(),
        P("dp", "ctx"),
    )
    out_specs = (P("dp", "ctx", "fsdp"), P("dp", "ctx", "fsdp"), P("dp", "ctx", "fsdp"), P())
    return jax.shard_map(shards, mesh=mesh, in_specs=in_specs, out_specs=out_specs, check_vma=False)
```

```python
import jax
import jax.numpy as jnp
from jax import lax
from jax.sharding import PartitionSpec as P

HD = 128
HQ = 16
HK = 8
WINDOW = 1024
QSCALAR = 168


epsilon = 1e-06


def passed_along(value, axis, steps):
    count = lax.axis_size(axis)
    initial, last = (max(0, -steps), min(count, count - steps))
    return lax.ppermute(value, axis, [(source, source + steps) for source in range(initial, last)])


def exchanged_sum(value, axis, stride):
    count = lax.axis_size(axis)
    return value + lax.ppermute(value, axis, [(source, source ^ stride) for source in range(count)])


def three_way_sum(value, axis, stride):
    count = lax.axis_size(axis)
    digit = (lax.axis_index(axis) // stride) % 3
    received = [value]
    for shift in (1, 2):
        pairs = []
        for source in range(count):
            place = (source // stride) % 3
            pairs.append((source, source + ((place + shift) % 3 - place) * stride))
        received.append(lax.ppermute(value, axis, pairs))
    ordered = []
    for place in range(3):
        pick = received[0]
        for shift in (1, 2):
            pick = jnp.where((digit - shift) % 3 == place, received[shift], pick)
        pick = jnp.where(digit == place, received[0], pick)
        ordered.append(pick)
    return ordered[0] + ordered[1] + ordered[2]


def total_over_devices(value):
    value = exchanged_sum(value, "fsdp", 1)
    value = exchanged_sum(value, "fsdp", 2)
    value = exchanged_sum(value, "dp", 1)
    for stride in (1, 2, 4, 8, 16):
        value = exchanged_sum(value, "ctx", stride)
    return three_way_sum(value, "ctx", 32)


def normalize(raw, gain, factor):
    values = raw.astype(jnp.float32)
    inverse = lax.rsqrt(jnp.mean(values * values, axis=-1, keepdims=True) + epsilon)
    unit_rows = values * inverse
    return (unit_rows, inverse, (unit_rows * gain * factor).astype(jnp.bfloat16))


def norm_backward(grad_n, unit_rows, inverse, gain, factor):
    grad_hat = grad_n * gain * factor
    return (grad_hat - unit_rows * jnp.mean(grad_hat * unit_rows, axis=-1, keepdims=True)) * inverse


def shards(query, key, value, out_grad, query_gain, key_gain, list_start):
    tokens = query.shape[1]
    kv_heads = key.shape[2] // HD
    group_size = query.shape[2] // key.shape[2]
    factor = QSCALAR ** (-0.5)
    reach = WINDOW // tokens
    query_hat, query_inv, query_n = normalize(
        query[0].reshape(tokens, kv_heads, group_size, HD), query_gain, factor
    )
    key_raw = key[0].reshape(tokens, kv_heads, HD)
    key_hat, key_inv, key_n = normalize(key_raw, key_gain, 1.0)
    own_values = value[0].reshape(tokens, kv_heads, HD)
    grads_in = out_grad[0].reshape(tokens, kv_heads, group_size, HD)
    starts = list_start[0]
    anchor = lax.axis_index("ctx") * tokens
    query_place = anchor + jnp.arange(tokens, dtype=jnp.int32)
    packed = jnp.concatenate([key_raw, own_values], axis=-1)
    blocks = [(key_n, own_values)]
    block_hats = [key_hat]
    for distance in range(1, reach + 1):
        arrived = passed_along(packed, "ctx", distance)
        arrived_hat, _, arrived_n = normalize(arrived[..., :HD], key_gain, 1.0)
        blocks.append((arrived_n, arrived[..., HD:]))
        block_hats.append(arrived_hat)
    allowed_sets = []
    for distance in range(reach + 1):
        key_place = anchor - distance * tokens + jnp.arange(tokens, dtype=jnp.int32)
        allowed_sets.append(
            (key_place[None, :] >= starts[:, None])
            & (key_place[None, :] <= query_place[:, None])
            & (query_place[:, None] - key_place[None, :] < WINDOW)
        )

    def forward_block(operands):
        allowed, key_block = operands
        scores = jnp.einsum(
            "tkgd,ukd->kgtu", query_n, key_block, preferred_element_type=jnp.float32
        )
        return jnp.where(allowed[None, None], jnp.exp(scores), 0.0)

    cached = [forward_block((allowed_sets[index], blocks[index][0])) for index in range(reach + 1)]
    denominator = jnp.sum(cached[0], axis=-1, keepdims=True)
    for weight in cached[1:]:
        denominator = denominator + jnp.sum(weight, axis=-1, keepdims=True)
    weights_bf = [(weight / denominator).astype(jnp.bfloat16) for weight in cached]
    attend_zero = jnp.zeros((tokens, kv_heads, group_size, HD), jnp.float32)
    attended = attend_zero
    for index in range(reach + 1):
        attend_prob = weights_bf[index]
        attend_value_block = blocks[index][1]
        attended = attended + jnp.einsum(
            "kgtu,ukd->tkgd", attend_prob, attend_value_block, preferred_element_type=jnp.float32
        )
    row_term = jnp.transpose(jnp.sum(grads_in.astype(jnp.float32) * attended, axis=-1), (1, 2, 0))[
        ..., None
    ]
    dquery_n = attend_zero
    pieces = []
    for index in range(reach + 1):
        prob = weights_bf[index]
        backward_key_block = blocks[index][0]
        value_block = blocks[index][1]
        products = jnp.einsum(
            "tkgd,ukd->kgtu", grads_in, value_block, preferred_element_type=jnp.float32
        )
        dscore = (prob.astype(jnp.float32) * (products - row_term)).astype(jnp.bfloat16)
        dquery_part = jnp.einsum(
            "kgtu,ukd->tkgd", dscore, backward_key_block, preferred_element_type=jnp.float32
        )
        dkey_part = jnp.einsum(
            "kgtu,tkgd->ukd", dscore, query_n, preferred_element_type=jnp.float32
        )
        dvalue_part = jnp.einsum(
            "kgtu,tkgd->ukd", prob, grads_in, preferred_element_type=jnp.float32
        )
        dquery_n = dquery_n + dquery_part
        pieces.append((dkey_part, dvalue_part))
    key_term = jnp.sum(pieces[0][0] * block_hats[0], axis=(0, 1))
    for distance in range(1, reach + 1):
        key_term = key_term + jnp.sum(pieces[distance][0] * block_hats[distance], axis=(0, 1))
    partial_sums = jnp.stack([jnp.sum(dquery_n * query_hat, axis=(0, 1, 2)) * factor, key_term])
    summed = total_over_devices(partial_sums)
    returns = [
        passed_along(
            jnp.concatenate(pieces[distance], axis=-1).astype(jnp.bfloat16), "ctx", -distance
        ).astype(jnp.float32)
        for distance in range(1, reach + 1)
    ]
    summed, *returns = lax.optimization_barrier((summed, *returns))
    dkey_n = pieces[0][0]
    dvalue_sum = pieces[0][1]
    for returned in returns:
        dkey_n = dkey_n + returned[..., :HD]
        dvalue_sum = dvalue_sum + returned[..., HD:]
    query_grad = (
        norm_backward(dquery_n, query_hat, query_inv, query_gain, factor)
        .astype(jnp.bfloat16)
        .reshape(1, tokens, -1)
    )
    key_grad = (
        norm_backward(dkey_n, key_hat, key_inv, key_gain, 1.0)
        .astype(jnp.bfloat16)
        .reshape(1, tokens, -1)
    )
    value_grad = dvalue_sum.astype(jnp.bfloat16).reshape(1, tokens, -1)
    counted = lax.axis_size("dp") * lax.axis_size("ctx") * tokens
    normalizers = jnp.array([[(counted * HQ) ** (-0.5)], [(counted * HK) ** (-0.5)]], jnp.float32)
    return (query_grad, key_grad, value_grad, summed * normalizers)


def solution(mesh):
    in_specs = (
        P("dp", "ctx", "fsdp"),
        P("dp", "ctx", "fsdp"),
        P("dp", "ctx", "fsdp"),
        P("dp", "ctx", "fsdp"),
        P(),
        P(),
        P("dp", "ctx"),
    )
    out_specs = (P("dp", "ctx", "fsdp"), P("dp", "ctx", "fsdp"), P("dp", "ctx", "fsdp"), P())
    return jax.shard_map(shards, mesh=mesh, in_specs=in_specs, out_specs=out_specs, check_vma=False)
```

```python
import jax
import jax.numpy as jnp
from jax import lax
from jax.sharding import PartitionSpec as P

HD = 128
HQ = 16
HK = 8
WINDOW = 1024
QSCALAR = 168


epsilon = 1e-06


def passed_along(value, axis, steps):
    count = lax.axis_size(axis)
    initial, last = (max(0, -steps), min(count, count - steps))
    return lax.ppermute(value, axis, [(source, source + steps) for source in range(initial, last)])


def exchanged_sum(value, axis, stride):
    count = lax.axis_size(axis)
    return value + lax.ppermute(value, axis, [(source, source ^ stride) for source in range(count)])


def three_way_sum(value, axis, stride):
    count = lax.axis_size(axis)
    digit = (lax.axis_index(axis) // stride) % 3
    received = [value]
    for shift in (1, 2):
        pairs = []
        for source in range(count):
            place = (source // stride) % 3
            pairs.append((source, source + ((place + shift) % 3 - place) * stride))
        received.append(lax.ppermute(value, axis, pairs))
    ordered = []
    for place in range(3):
        pick = received[0]
        for shift in (1, 2):
            pick = jnp.where((digit - shift) % 3 == place, received[shift], pick)
        pick = jnp.where(digit == place, received[0], pick)
        ordered.append(pick)
    return ordered[0] + ordered[1] + ordered[2]


def total_over_devices(value):
    value = exchanged_sum(value, "fsdp", 1)
    value = exchanged_sum(value, "fsdp", 2)
    value = exchanged_sum(value, "dp", 1)
    for stride in (1, 2, 4, 8, 16):
        value = exchanged_sum(value, "ctx", stride)
    return three_way_sum(value, "ctx", 32)


def normalize(raw, gain, factor):
    values = raw.astype(jnp.float32)
    inverse = lax.rsqrt(jnp.mean(values * values, axis=-1, keepdims=True) + epsilon)
    unit_rows = values * inverse
    return (unit_rows, inverse, (unit_rows * gain * factor).astype(jnp.bfloat16))


def norm_backward(grad_n, unit_rows, inverse, gain, factor):
    grad_hat = grad_n * gain * factor
    return (grad_hat - unit_rows * jnp.mean(grad_hat * unit_rows, axis=-1, keepdims=True)) * inverse


def shards(query, key, value, out_grad, query_gain, key_gain, list_start):
    tokens = query.shape[1]
    kv_heads = key.shape[2] // HD
    group_size = query.shape[2] // key.shape[2]
    factor = QSCALAR ** (-0.5)
    reach = WINDOW // tokens
    query_hat, query_inv, query_n = normalize(
        query[0].reshape(tokens, kv_heads, group_size, HD), query_gain, factor
    )
    key_raw = key[0].reshape(tokens, kv_heads, HD)
    key_hat, key_inv, key_n = normalize(key_raw, key_gain, 1.0)
    own_values = value[0].reshape(tokens, kv_heads, HD)
    grads_in = out_grad[0].reshape(tokens, kv_heads, group_size, HD)
    starts = list_start[0]
    anchor = lax.axis_index("ctx") * tokens
    query_place = anchor + jnp.arange(tokens, dtype=jnp.int32)
    packed = jnp.concatenate([key_raw, own_values], axis=-1)
    blocks = [(key_n, own_values)]
    block_hats = [key_hat]
    for distance in range(1, reach + 1):
        arrived = passed_along(packed, "ctx", distance)
        arrived_hat, _, arrived_n = normalize(arrived[..., :HD], key_gain, 1.0)
        blocks.append((arrived_n, arrived[..., HD:]))
        block_hats.append(arrived_hat)
    allowed_sets = []
    for distance in range(reach + 1):
        key_place = anchor - distance * tokens + jnp.arange(tokens, dtype=jnp.int32)
        allowed_sets.append(
            (key_place[None, :] >= starts[:, None])
            & (key_place[None, :] <= query_place[:, None])
            & (query_place[:, None] - key_place[None, :] < WINDOW)
        )

    def forward_block(operands):
        allowed, key_block = operands
        scores = jnp.einsum(
            "tkgd,ukd->kgtu", query_n, key_block, preferred_element_type=jnp.float32
        )
        return jnp.where(allowed[None, None], jnp.exp(scores), 0.0)

    cached = [forward_block((allowed_sets[index], blocks[index][0])) for index in range(reach + 1)]
    denominator = jnp.sum(cached[0], axis=-1, keepdims=True)
    for weight in cached[1:]:
        denominator = denominator + jnp.sum(weight, axis=-1, keepdims=True)
    again_query_n = lax.optimization_barrier(query_n)
    weights_bf = []
    for index in range(reach + 1):
        scores = jnp.einsum(
            "tkgd,ukd->kgtu", again_query_n, blocks[index][0], preferred_element_type=jnp.float32
        )
        weight = jnp.where(allowed_sets[index][None, None], jnp.exp(scores), 0.0)
        weights_bf.append((weight / denominator).astype(jnp.bfloat16))
    attend_zero = jnp.zeros((tokens, kv_heads, group_size, HD), jnp.float32)
    attended = attend_zero
    for index in range(reach + 1):
        attend_prob = weights_bf[index]
        attend_value_block = blocks[index][1]
        attended = attended + jnp.einsum(
            "kgtu,ukd->tkgd", attend_prob, attend_value_block, preferred_element_type=jnp.float32
        )
    row_term = jnp.transpose(jnp.sum(grads_in.astype(jnp.float32) * attended, axis=-1), (1, 2, 0))[
        ..., None
    ]
    dquery_n = attend_zero
    pieces = []
    for index in range(reach + 1):
        prob = weights_bf[index]
        backward_key_block = blocks[index][0]
        value_block = blocks[index][1]
        products = jnp.einsum(
            "tkgd,ukd->kgtu", grads_in, value_block, preferred_element_type=jnp.float32
        )
        dscore = (prob.astype(jnp.float32) * (products - row_term)).astype(jnp.bfloat16)
        dquery_part = jnp.einsum(
            "kgtu,ukd->tkgd", dscore, backward_key_block, preferred_element_type=jnp.float32
        )
        dkey_part = jnp.einsum(
            "kgtu,tkgd->ukd", dscore, query_n, preferred_element_type=jnp.float32
        )
        dvalue_part = jnp.einsum(
            "kgtu,tkgd->ukd", prob, grads_in, preferred_element_type=jnp.float32
        )
        dquery_n = dquery_n + dquery_part
        pieces.append((dkey_part, dvalue_part))
    key_term = jnp.sum(pieces[0][0] * block_hats[0], axis=(0, 1))
    for distance in range(1, reach + 1):
        key_term = key_term + jnp.sum(pieces[distance][0] * block_hats[distance], axis=(0, 1))
    partial_sums = jnp.stack([jnp.sum(dquery_n * query_hat, axis=(0, 1, 2)) * factor, key_term])
    summed = total_over_devices(partial_sums)
    returns = [
        passed_along(
            jnp.concatenate(pieces[distance], axis=-1).astype(jnp.bfloat16), "ctx", -distance
        ).astype(jnp.float32)
        for distance in range(1, reach + 1)
    ]
    summed, *returns = lax.optimization_barrier((summed, *returns))
    dkey_n = pieces[0][0]
    dvalue_sum = pieces[0][1]
    for returned in returns:
        dkey_n = dkey_n + returned[..., :HD]
        dvalue_sum = dvalue_sum + returned[..., HD:]
    query_grad = (
        norm_backward(dquery_n, query_hat, query_inv, query_gain, factor)
        .astype(jnp.bfloat16)
        .reshape(1, tokens, -1)
    )
    key_grad = (
        norm_backward(dkey_n, key_hat, key_inv, key_gain, 1.0)
        .astype(jnp.bfloat16)
        .reshape(1, tokens, -1)
    )
    value_grad = dvalue_sum.astype(jnp.bfloat16).reshape(1, tokens, -1)
    counted = lax.axis_size("dp") * lax.axis_size("ctx") * tokens
    normalizers = jnp.array([[(counted * HQ) ** (-0.5)], [(counted * HK) ** (-0.5)]], jnp.float32)
    return (query_grad, key_grad, value_grad, summed * normalizers)


def solution(mesh):
    in_specs = (
        P("dp", "ctx", "fsdp"),
        P("dp", "ctx", "fsdp"),
        P("dp", "ctx", "fsdp"),
        P("dp", "ctx", "fsdp"),
        P(),
        P(),
        P("dp", "ctx"),
    )
    out_specs = (P("dp", "ctx", "fsdp"), P("dp", "ctx", "fsdp"), P("dp", "ctx", "fsdp"), P())
    return jax.shard_map(shards, mesh=mesh, in_specs=in_specs, out_specs=out_specs, check_vma=False)
```

```python
import jax
import jax.numpy as jnp
from jax import lax
from jax.sharding import PartitionSpec as P

HD = 128
HQ = 16
HK = 8
WINDOW = 1024
QSCALAR = 168


epsilon = 1e-06


def passed_along(value, axis, steps):
    count = lax.axis_size(axis)
    initial, last = (max(0, -steps), min(count, count - steps))
    return lax.ppermute(value, axis, [(source, source + steps) for source in range(initial, last)])


def exchanged_sum(value, axis, stride):
    count = lax.axis_size(axis)
    return value + lax.ppermute(value, axis, [(source, source ^ stride) for source in range(count)])


def three_way_sum(value, axis, stride):
    count = lax.axis_size(axis)
    digit = (lax.axis_index(axis) // stride) % 3
    received = [value]
    for shift in (1, 2):
        pairs = []
        for source in range(count):
            place = (source // stride) % 3
            pairs.append((source, source + ((place + shift) % 3 - place) * stride))
        received.append(lax.ppermute(value, axis, pairs))
    ordered = []
    for place in range(3):
        pick = received[0]
        for shift in (1, 2):
            pick = jnp.where((digit - shift) % 3 == place, received[shift], pick)
        pick = jnp.where(digit == place, received[0], pick)
        ordered.append(pick)
    return ordered[0] + ordered[1] + ordered[2]


def total_over_devices(value):
    value = exchanged_sum(value, "fsdp", 1)
    value = exchanged_sum(value, "fsdp", 2)
    value = exchanged_sum(value, "dp", 1)
    for stride in (1, 2, 4, 8, 16):
        value = exchanged_sum(value, "ctx", stride)
    return three_way_sum(value, "ctx", 32)


def normalize(raw, gain, factor):
    values = raw.astype(jnp.float32)
    inverse = lax.rsqrt(jnp.mean(values * values, axis=-1, keepdims=True) + epsilon)
    unit_rows = values * inverse
    return (unit_rows, inverse, (unit_rows * gain * factor).astype(jnp.bfloat16))


def norm_backward(grad_n, unit_rows, inverse, gain, factor):
    grad_hat = grad_n * gain * factor
    return (grad_hat - unit_rows * jnp.mean(grad_hat * unit_rows, axis=-1, keepdims=True)) * inverse


def shards(query, key, value, out_grad, query_gain, key_gain, list_start):
    tokens = query.shape[1]
    kv_heads = key.shape[2] // HD
    group_size = query.shape[2] // key.shape[2]
    factor = QSCALAR ** (-0.5)
    reach = WINDOW // tokens
    query_hat, query_inv, query_n = normalize(
        query[0].reshape(tokens, kv_heads, group_size, HD), query_gain, factor
    )
    key_raw = key[0].reshape(tokens, kv_heads, HD)
    key_hat, key_inv, key_n = normalize(key_raw, key_gain, 1.0)
    own_values = value[0].reshape(tokens, kv_heads, HD)
    grads_in = out_grad[0].reshape(tokens, kv_heads, group_size, HD)
    starts = list_start[0]
    anchor = lax.axis_index("ctx") * tokens
    query_place = anchor + jnp.arange(tokens, dtype=jnp.int32)
    packed = jnp.concatenate([key_raw, own_values], axis=-1)
    blocks = [(key_n, own_values)]
    block_hats = [key_hat]
    for distance in range(1, reach + 1):
        arrived = passed_along(packed, "ctx", distance)
        arrived_hat, _, arrived_n = normalize(arrived[..., :HD], key_gain, 1.0)
        blocks.append((arrived_n, arrived[..., HD:]))
        block_hats.append(arrived_hat)
    allowed_sets = []
    for distance in range(reach + 1):
        key_place = anchor - distance * tokens + jnp.arange(tokens, dtype=jnp.int32)
        allowed_sets.append(
            (key_place[None, :] >= starts[:, None])
            & (key_place[None, :] <= query_place[:, None])
            & (query_place[:, None] - key_place[None, :] < WINDOW)
        )

    def forward_block(operands):
        allowed, key_block = operands
        scores = jnp.einsum(
            "tkgd,ukd->kgtu", query_n, key_block, preferred_element_type=jnp.float32
        )
        return jnp.where(allowed[None, None], jnp.exp(scores), 0.0)

    cached = [forward_block((allowed_sets[index], blocks[index][0])) for index in range(reach + 1)]
    denominator = jnp.sum(cached[0], axis=-1, keepdims=True)
    for weight in cached[1:]:
        denominator = denominator + jnp.sum(weight, axis=-1, keepdims=True)
    weights_bf = [(weight / denominator).astype(jnp.bfloat16) for weight in cached]
    attend_zero = jnp.zeros((tokens, kv_heads, group_size, HD), jnp.float32)
    attended = attend_zero
    for index in range(reach + 1):
        attend_prob = weights_bf[index]
        attend_value_block = blocks[index][1]
        attended = attended + jnp.einsum(
            "kgtu,ukd->tkgd", attend_prob, attend_value_block, preferred_element_type=jnp.float32
        )
    row_term = jnp.transpose(jnp.sum(grads_in.astype(jnp.float32) * attended, axis=-1), (1, 2, 0))[
        ..., None
    ]
    dquery_n = attend_zero
    pieces = []
    for index in range(reach + 1):
        prob = weights_bf[index]
        backward_key_block = blocks[index][0]
        value_block = blocks[index][1]
        products = jnp.einsum(
            "tkgd,ukd->kgtu", grads_in, value_block, preferred_element_type=jnp.float32
        )
        dscore = (prob.astype(jnp.float32) * (products - row_term)).astype(jnp.bfloat16)
        dquery_part = jnp.einsum(
            "kgtu,ukd->tkgd", dscore, backward_key_block, preferred_element_type=jnp.float32
        )
        dkey_part = jnp.einsum(
            "kgtu,tkgd->ukd", dscore, query_n, preferred_element_type=jnp.float32
        )
        dvalue_part = jnp.einsum(
            "kgtu,tkgd->ukd", prob, grads_in, preferred_element_type=jnp.float32
        )
        dquery_n = dquery_n + dquery_part
        pieces.append((dkey_part, dvalue_part))
    key_term = jnp.sum(pieces[0][0] * block_hats[0], axis=(0, 1))
    for distance in range(1, reach + 1):
        key_term = key_term + jnp.sum(pieces[distance][0] * block_hats[distance], axis=(0, 1))
    partial_sums = jnp.stack([jnp.sum(dquery_n * query_hat, axis=(0, 1, 2)) * factor, key_term])
    summed = total_over_devices(partial_sums)
    returns = [
        passed_along(
            jnp.concatenate(pieces[distance], axis=-1).astype(jnp.bfloat16), "ctx", -distance
        )
        for distance in range(1, reach + 1)
    ]
    summed, *returns = lax.optimization_barrier((summed, *returns))
    dkey_n = pieces[0][0]
    dvalue_sum = pieces[0][1]
    for returned in returns:
        dkey_n = dkey_n + returned[..., :HD].astype(jnp.float32)
        dvalue_sum = dvalue_sum + returned[..., HD:].astype(jnp.float32)
    query_grad = (
        norm_backward(dquery_n, query_hat, query_inv, query_gain, factor)
        .astype(jnp.bfloat16)
        .reshape(1, tokens, -1)
    )
    key_grad = (
        norm_backward(dkey_n, key_hat, key_inv, key_gain, 1.0)
        .astype(jnp.bfloat16)
        .reshape(1, tokens, -1)
    )
    value_grad = dvalue_sum.astype(jnp.bfloat16).reshape(1, tokens, -1)
    counted = lax.axis_size("dp") * lax.axis_size("ctx") * tokens
    normalizers = jnp.array([[(counted * HQ) ** (-0.5)], [(counted * HK) ** (-0.5)]], jnp.float32)
    return (query_grad, key_grad, value_grad, summed * normalizers)


def solution(mesh):
    in_specs = (
        P("dp", "ctx", "fsdp"),
        P("dp", "ctx", "fsdp"),
        P("dp", "ctx", "fsdp"),
        P("dp", "ctx", "fsdp"),
        P(),
        P(),
        P("dp", "ctx"),
    )
    out_specs = (P("dp", "ctx", "fsdp"), P("dp", "ctx", "fsdp"), P("dp", "ctx", "fsdp"), P())
    return jax.shard_map(shards, mesh=mesh, in_specs=in_specs, out_specs=out_specs, check_vma=False)
```

```python
import jax
import jax.numpy as jnp
from jax import lax
from jax.sharding import PartitionSpec as P

HD = 128
HQ = 16
HK = 8
WINDOW = 1024
QSCALAR = 168


epsilon = 1e-06


def passed_along(value, axis, steps):
    count = lax.axis_size(axis)
    initial, last = (max(0, -steps), min(count, count - steps))
    return lax.ppermute(value, axis, [(source, source + steps) for source in range(initial, last)])


def exchanged_sum(value, axis, stride):
    count = lax.axis_size(axis)
    return value + lax.ppermute(value, axis, [(source, source ^ stride) for source in range(count)])


def three_way_sum(value, axis, stride):
    count = lax.axis_size(axis)
    digit = (lax.axis_index(axis) // stride) % 3
    received = [value]
    for shift in (1, 2):
        pairs = []
        for source in range(count):
            place = (source // stride) % 3
            pairs.append((source, source + ((place + shift) % 3 - place) * stride))
        received.append(lax.ppermute(value, axis, pairs))
    ordered = []
    for place in range(3):
        pick = received[0]
        for shift in (1, 2):
            pick = jnp.where((digit - shift) % 3 == place, received[shift], pick)
        pick = jnp.where(digit == place, received[0], pick)
        ordered.append(pick)
    return ordered[0] + ordered[1] + ordered[2]


def total_over_devices(value):
    value = exchanged_sum(value, "fsdp", 1)
    value = exchanged_sum(value, "fsdp", 2)
    value = exchanged_sum(value, "dp", 1)
    for stride in (1, 2, 4, 8):
        value = exchanged_sum(value, "ctx", stride)
    value = three_way_sum(value, "ctx", 16)
    count = lax.axis_size("ctx")
    half = count // 2
    return value + lax.ppermute(value, "ctx", [(source, (source + half) % count) for source in range(count)])


def normalize(raw, gain, factor):
    values = raw.astype(jnp.float32)
    inverse = lax.rsqrt(jnp.mean(values * values, axis=-1, keepdims=True) + epsilon)
    unit_rows = values * inverse
    return (unit_rows, inverse, (unit_rows * gain * factor).astype(jnp.bfloat16))


def norm_backward(grad_n, unit_rows, inverse, gain, factor):
    grad_hat = grad_n * gain * factor
    return (grad_hat - unit_rows * jnp.mean(grad_hat * unit_rows, axis=-1, keepdims=True)) * inverse


def shards(query, key, value, out_grad, query_gain, key_gain, list_start):
    tokens = query.shape[1]
    kv_heads = key.shape[2] // HD
    group_size = query.shape[2] // key.shape[2]
    factor = QSCALAR ** (-0.5)
    reach = WINDOW // tokens
    query_hat, query_inv, query_n = normalize(
        query[0].reshape(tokens, kv_heads, group_size, HD), query_gain, factor
    )
    key_raw = key[0].reshape(tokens, kv_heads, HD)
    key_hat, key_inv, key_n = normalize(key_raw, key_gain, 1.0)
    own_values = value[0].reshape(tokens, kv_heads, HD)
    grads_in = out_grad[0].reshape(tokens, kv_heads, group_size, HD)
    starts = list_start[0]
    anchor = lax.axis_index("ctx") * tokens
    query_place = anchor + jnp.arange(tokens, dtype=jnp.int32)
    packed = jnp.concatenate([key_raw, own_values], axis=-1)
    blocks = [(key_n, own_values)]
    block_hats = [key_hat]
    for distance in range(1, reach + 1):
        arrived = passed_along(packed, "ctx", distance)
        arrived_hat, _, arrived_n = normalize(arrived[..., :HD], key_gain, 1.0)
        blocks.append((arrived_n, arrived[..., HD:]))
        block_hats.append(arrived_hat)
    allowed_sets = []
    for distance in range(reach + 1):
        key_place = anchor - distance * tokens + jnp.arange(tokens, dtype=jnp.int32)
        allowed_sets.append(
            (key_place[None, :] >= starts[:, None])
            & (key_place[None, :] <= query_place[:, None])
            & (query_place[:, None] - key_place[None, :] < WINDOW)
        )

    def forward_block(operands):
        allowed, key_block = operands
        scores = jnp.einsum(
            "tkgd,ukd->kgtu", query_n, key_block, preferred_element_type=jnp.float32
        )
        return jnp.where(allowed[None, None], jnp.exp(scores), 0.0)

    cached = [forward_block((allowed_sets[index], blocks[index][0])) for index in range(reach + 1)]
    denominator = jnp.sum(cached[0], axis=-1, keepdims=True)
    for weight in cached[1:]:
        denominator = denominator + jnp.sum(weight, axis=-1, keepdims=True)
    weights_bf = [(weight / denominator).astype(jnp.bfloat16) for weight in cached]
    attend_zero = jnp.zeros((tokens, kv_heads, group_size, HD), jnp.float32)
    attended = attend_zero
    for index in range(reach + 1):
        attend_prob = weights_bf[index]
        attend_value_block = blocks[index][1]
        attended = attended + jnp.einsum(
            "kgtu,ukd->tkgd", attend_prob, attend_value_block, preferred_element_type=jnp.float32
        )
    row_term = jnp.transpose(jnp.sum(grads_in.astype(jnp.float32) * attended, axis=-1), (1, 2, 0))[
        ..., None
    ]
    dquery_n = attend_zero
    pieces = []
    for index in range(reach + 1):
        prob = weights_bf[index]
        backward_key_block = blocks[index][0]
        value_block = blocks[index][1]
        products = jnp.einsum(
            "tkgd,ukd->kgtu", grads_in, value_block, preferred_element_type=jnp.float32
        )
        dscore = (prob.astype(jnp.float32) * (products - row_term)).astype(jnp.bfloat16)
        dquery_part = jnp.einsum(
            "kgtu,ukd->tkgd", dscore, backward_key_block, preferred_element_type=jnp.float32
        )
        dkey_part = jnp.einsum(
            "kgtu,tkgd->ukd", dscore, query_n, preferred_element_type=jnp.float32
        )
        dvalue_part = jnp.einsum(
            "kgtu,tkgd->ukd", prob, grads_in, preferred_element_type=jnp.float32
        )
        dquery_n = dquery_n + dquery_part
        pieces.append((dkey_part, dvalue_part))
    key_term = jnp.sum(pieces[0][0] * block_hats[0], axis=(0, 1))
    for distance in range(1, reach + 1):
        key_term = key_term + jnp.sum(pieces[distance][0] * block_hats[distance], axis=(0, 1))
    partial_sums = jnp.stack([jnp.sum(dquery_n * query_hat, axis=(0, 1, 2)) * factor, key_term])
    summed = total_over_devices(partial_sums)
    returns = [
        passed_along(
            jnp.concatenate(pieces[distance], axis=-1).astype(jnp.bfloat16), "ctx", -distance
        )
        for distance in range(1, reach + 1)
    ]
    summed, *returns = lax.optimization_barrier((summed, *returns))
    dkey_n = pieces[0][0]
    dvalue_sum = pieces[0][1]
    for returned in returns:
        dkey_n = dkey_n + returned[..., :HD].astype(jnp.float32)
        dvalue_sum = dvalue_sum + returned[..., HD:].astype(jnp.float32)
    query_grad = (
        norm_backward(dquery_n, query_hat, query_inv, query_gain, factor)
        .astype(jnp.bfloat16)
        .reshape(1, tokens, -1)
    )
    key_grad = (
        norm_backward(dkey_n, key_hat, key_inv, key_gain, 1.0)
        .astype(jnp.bfloat16)
        .reshape(1, tokens, -1)
    )
    value_grad = dvalue_sum.astype(jnp.bfloat16).reshape(1, tokens, -1)
    counted = lax.axis_size("dp") * lax.axis_size("ctx") * tokens
    normalizers = jnp.array([[(counted * HQ) ** (-0.5)], [(counted * HK) ** (-0.5)]], jnp.float32)
    return (query_grad, key_grad, value_grad, summed * normalizers)


def solution(mesh):
    in_specs = (
        P("dp", "ctx", "fsdp"),
        P("dp", "ctx", "fsdp"),
        P("dp", "ctx", "fsdp"),
        P("dp", "ctx", "fsdp"),
        P(),
        P(),
        P("dp", "ctx"),
    )
    out_specs = (P("dp", "ctx", "fsdp"), P("dp", "ctx", "fsdp"), P("dp", "ctx", "fsdp"), P())
    return jax.shard_map(shards, mesh=mesh, in_specs=in_specs, out_specs=out_specs, check_vma=False)
```

```python
import jax
import jax.numpy as jnp
from jax import lax
from jax.sharding import PartitionSpec as P

HD = 128
HQ = 16
HK = 8
WINDOW = 1024
QSCALAR = 168


epsilon = 1e-06


def passed_along(value, axis, steps):
    count = lax.axis_size(axis)
    initial, last = (max(0, -steps), min(count, count - steps))
    return lax.ppermute(value, axis, [(source, source + steps) for source in range(initial, last)])


def exchanged_sum(value, axis, stride):
    count = lax.axis_size(axis)
    return value + lax.ppermute(value, axis, [(source, source ^ stride) for source in range(count)])


def three_way_sum(value, axis, stride):
    count = lax.axis_size(axis)
    digit = (lax.axis_index(axis) // stride) % 3
    received = [value]
    for shift in (1, 2):
        pairs = []
        for source in range(count):
            place = (source // stride) % 3
            pairs.append((source, source + ((place + shift) % 3 - place) * stride))
        received.append(lax.ppermute(value, axis, pairs))
    ordered = []
    for place in range(3):
        pick = received[0]
        for shift in (1, 2):
            pick = jnp.where((digit - shift) % 3 == place, received[shift], pick)
        pick = jnp.where(digit == place, received[0], pick)
        ordered.append(pick)
    return ordered[0] + ordered[1] + ordered[2]


def first_rounds(value):
    value = exchanged_sum(value, "fsdp", 1)
    value = exchanged_sum(value, "fsdp", 2)
    value = exchanged_sum(value, "dp", 1)
    for stride in (1, 2):
        value = exchanged_sum(value, "ctx", stride)
    return value


def middle_rounds(value):
    for stride in (4, 8):
        value = exchanged_sum(value, "ctx", stride)
    return three_way_sum(value, "ctx", 16)


def last_round(value):
    count = lax.axis_size("ctx")
    half = count // 2
    return value + lax.ppermute(value, "ctx", [(source, (source + half) % count) for source in range(count)])


def normalize(raw, gain, factor):
    values = raw.astype(jnp.float32)
    inverse = lax.rsqrt(jnp.mean(values * values, axis=-1, keepdims=True) + epsilon)
    unit_rows = values * inverse
    return (unit_rows, inverse, (unit_rows * gain * factor).astype(jnp.bfloat16))


def norm_backward(grad_n, unit_rows, inverse, gain, factor):
    grad_hat = grad_n * gain * factor
    return (grad_hat - unit_rows * jnp.mean(grad_hat * unit_rows, axis=-1, keepdims=True)) * inverse


def shards(query, key, value, out_grad, query_gain, key_gain, list_start):
    tokens = query.shape[1]
    kv_heads = key.shape[2] // HD
    group_size = query.shape[2] // key.shape[2]
    factor = QSCALAR ** (-0.5)
    reach = WINDOW // tokens
    query_hat, query_inv, query_n = normalize(
        query[0].reshape(tokens, kv_heads, group_size, HD), query_gain, factor
    )
    key_raw = key[0].reshape(tokens, kv_heads, HD)
    key_hat, key_inv, key_n = normalize(key_raw, key_gain, 1.0)
    own_values = value[0].reshape(tokens, kv_heads, HD)
    grads_in = out_grad[0].reshape(tokens, kv_heads, group_size, HD)
    starts = list_start[0]
    anchor = lax.axis_index("ctx") * tokens
    query_place = anchor + jnp.arange(tokens, dtype=jnp.int32)
    packed = jnp.concatenate([key_raw, own_values], axis=-1)
    blocks = [(key_n, own_values)]
    block_hats = [key_hat]
    for distance in range(1, reach + 1):
        arrived = passed_along(packed, "ctx", distance)
        arrived_hat, _, arrived_n = normalize(arrived[..., :HD], key_gain, 1.0)
        blocks.append((arrived_n, arrived[..., HD:]))
        block_hats.append(arrived_hat)
    allowed_sets = []
    for distance in range(reach + 1):
        key_place = anchor - distance * tokens + jnp.arange(tokens, dtype=jnp.int32)
        allowed_sets.append(
            (key_place[None, :] >= starts[:, None])
            & (key_place[None, :] <= query_place[:, None])
            & (query_place[:, None] - key_place[None, :] < WINDOW)
        )

    def forward_block(operands):
        allowed, key_block = operands
        scores = jnp.einsum(
            "tkgd,ukd->kgtu", query_n, key_block, preferred_element_type=jnp.float32
        )
        return jnp.where(allowed[None, None], jnp.exp(scores), 0.0)

    cached = [forward_block((allowed_sets[index], blocks[index][0])) for index in range(reach + 1)]
    denominator = jnp.sum(cached[0], axis=-1, keepdims=True)
    for weight in cached[1:]:
        denominator = denominator + jnp.sum(weight, axis=-1, keepdims=True)
    weights_bf = [(weight / denominator).astype(jnp.bfloat16) for weight in cached]
    attend_zero = jnp.zeros((tokens, kv_heads, group_size, HD), jnp.float32)
    attended = attend_zero
    for index in range(reach + 1):
        attend_prob = weights_bf[index]
        attend_value_block = blocks[index][1]
        attended = attended + jnp.einsum(
            "kgtu,ukd->tkgd", attend_prob, attend_value_block, preferred_element_type=jnp.float32
        )
    row_term = jnp.transpose(jnp.sum(grads_in.astype(jnp.float32) * attended, axis=-1), (1, 2, 0))[
        ..., None
    ]
    dquery_n = attend_zero
    pieces = []
    for index in range(reach + 1):
        prob = weights_bf[index]
        backward_key_block = blocks[index][0]
        value_block = blocks[index][1]
        products = jnp.einsum(
            "tkgd,ukd->kgtu", grads_in, value_block, preferred_element_type=jnp.float32
        )
        dscore = (prob.astype(jnp.float32) * (products - row_term)).astype(jnp.bfloat16)
        dquery_part = jnp.einsum(
            "kgtu,ukd->tkgd", dscore, backward_key_block, preferred_element_type=jnp.float32
        )
        dkey_part = jnp.einsum(
            "kgtu,tkgd->ukd", dscore, query_n, preferred_element_type=jnp.float32
        )
        dvalue_part = jnp.einsum(
            "kgtu,tkgd->ukd", prob, grads_in, preferred_element_type=jnp.float32
        )
        dquery_n = dquery_n + dquery_part
        pieces.append((dkey_part, dvalue_part))
    key_term = jnp.sum(pieces[0][0] * block_hats[0], axis=(0, 1))
    for distance in range(1, reach + 1):
        key_term = key_term + jnp.sum(pieces[distance][0] * block_hats[distance], axis=(0, 1))
    partial_sums = jnp.stack([jnp.sum(dquery_n * query_hat, axis=(0, 1, 2)) * factor, key_term])
    returns = [
        passed_along(
            jnp.concatenate(pieces[distance], axis=-1).astype(jnp.bfloat16), "ctx", -distance
        )
        for distance in range(1, reach + 1)
    ]
    summed = first_rounds(partial_sums)
    summed, *returns = lax.optimization_barrier((summed, *returns))
    dkey_n = pieces[0][0]
    dvalue_sum = pieces[0][1]
    for returned in returns:
        dkey_n = dkey_n + returned[..., :HD].astype(jnp.float32)
        dvalue_sum = dvalue_sum + returned[..., HD:].astype(jnp.float32)
    query_grad = (
        norm_backward(dquery_n, query_hat, query_inv, query_gain, factor)
        .astype(jnp.bfloat16)
        .reshape(1, tokens, -1)
    )
    key_grad = (
        norm_backward(dkey_n, key_hat, key_inv, key_gain, 1.0)
        .astype(jnp.bfloat16)
        .reshape(1, tokens, -1)
    )
    value_grad = dvalue_sum.astype(jnp.bfloat16).reshape(1, tokens, -1)
    summed = middle_rounds(summed)
    summed, query_grad, key_grad, value_grad = lax.optimization_barrier(
        (summed, query_grad, key_grad, value_grad)
    )
    summed = last_round(summed)
    counted = lax.axis_size("dp") * lax.axis_size("ctx") * tokens
    normalizers = jnp.array([[(counted * HQ) ** (-0.5)], [(counted * HK) ** (-0.5)]], jnp.float32)
    return (query_grad, key_grad, value_grad, summed * normalizers)


def solution(mesh):
    in_specs = (
        P("dp", "ctx", "fsdp"),
        P("dp", "ctx", "fsdp"),
        P("dp", "ctx", "fsdp"),
        P("dp", "ctx", "fsdp"),
        P(),
        P(),
        P("dp", "ctx"),
    )
    out_specs = (P("dp", "ctx", "fsdp"), P("dp", "ctx", "fsdp"), P("dp", "ctx", "fsdp"), P())
    return jax.shard_map(shards, mesh=mesh, in_specs=in_specs, out_specs=out_specs, check_vma=False)
```

```python
import jax
import jax.numpy as jnp
from jax import lax
from jax.sharding import PartitionSpec as P

HD = 128
HQ = 16
HK = 8
WINDOW = 1024
QSCALAR = 168


epsilon = 1e-06


def passed_along(value, axis, steps):
    count = lax.axis_size(axis)
    initial, last = (max(0, -steps), min(count, count - steps))
    return lax.ppermute(value, axis, [(source, source + steps) for source in range(initial, last)])


def exchanged_sum(value, axis, stride):
    count = lax.axis_size(axis)
    return value + lax.ppermute(value, axis, [(source, source ^ stride) for source in range(count)])


def three_way_sum(value, axis, stride):
    count = lax.axis_size(axis)
    digit = (lax.axis_index(axis) // stride) % 3
    received = [value]
    for shift in (1, 2):
        pairs = []
        for source in range(count):
            place = (source // stride) % 3
            pairs.append((source, source + ((place + shift) % 3 - place) * stride))
        received.append(lax.ppermute(value, axis, pairs))
    ordered = []
    for place in range(3):
        pick = received[0]
        for shift in (1, 2):
            pick = jnp.where((digit - shift) % 3 == place, received[shift], pick)
        pick = jnp.where(digit == place, received[0], pick)
        ordered.append(pick)
    return ordered[0] + ordered[1] + ordered[2]


def first_rounds(value):
    value = exchanged_sum(value, "fsdp", 1)
    value = exchanged_sum(value, "fsdp", 2)
    value = exchanged_sum(value, "dp", 1)
    for stride in (1, 2):
        value = exchanged_sum(value, "ctx", stride)
    return value


def middle_rounds(value):
    for stride in (4, 8):
        value = exchanged_sum(value, "ctx", stride)
    return value


def last_round(value):
    value = three_way_sum(value, "ctx", 16)
    count = lax.axis_size("ctx")
    half = count // 2
    return value + lax.ppermute(value, "ctx", [(source, (source + half) % count) for source in range(count)])


def normalize(raw, gain, factor):
    values = raw.astype(jnp.float32)
    inverse = lax.rsqrt(jnp.mean(values * values, axis=-1, keepdims=True) + epsilon)
    unit_rows = values * inverse
    return (unit_rows, inverse, (unit_rows * gain * factor).astype(jnp.bfloat16))


def norm_backward(grad_n, unit_rows, inverse, gain, factor):
    grad_hat = grad_n * gain * factor
    return (grad_hat - unit_rows * jnp.mean(grad_hat * unit_rows, axis=-1, keepdims=True)) * inverse


def shards(query, key, value, out_grad, query_gain, key_gain, list_start):
    tokens = query.shape[1]
    kv_heads = key.shape[2] // HD
    group_size = query.shape[2] // key.shape[2]
    factor = QSCALAR ** (-0.5)
    reach = WINDOW // tokens
    query_hat, query_inv, query_n = normalize(
        query[0].reshape(tokens, kv_heads, group_size, HD), query_gain, factor
    )
    key_raw = key[0].reshape(tokens, kv_heads, HD)
    key_hat, key_inv, key_n = normalize(key_raw, key_gain, 1.0)
    own_values = value[0].reshape(tokens, kv_heads, HD)
    grads_in = out_grad[0].reshape(tokens, kv_heads, group_size, HD)
    starts = list_start[0]
    anchor = lax.axis_index("ctx") * tokens
    query_place = anchor + jnp.arange(tokens, dtype=jnp.int32)
    packed = jnp.concatenate([key_raw, own_values], axis=-1)
    blocks = [(key_n, own_values)]
    block_hats = [key_hat]
    for distance in range(1, reach + 1):
        arrived = passed_along(packed, "ctx", distance)
        arrived_hat, _, arrived_n = normalize(arrived[..., :HD], key_gain, 1.0)
        blocks.append((arrived_n, arrived[..., HD:]))
        block_hats.append(arrived_hat)
    allowed_sets = []
    for distance in range(reach + 1):
        key_place = anchor - distance * tokens + jnp.arange(tokens, dtype=jnp.int32)
        allowed_sets.append(
            (key_place[None, :] >= starts[:, None])
            & (key_place[None, :] <= query_place[:, None])
            & (query_place[:, None] - key_place[None, :] < WINDOW)
        )

    def forward_block(operands):
        allowed, key_block = operands
        scores = jnp.einsum(
            "tkgd,ukd->kgtu", query_n, key_block, preferred_element_type=jnp.float32
        )
        return jnp.where(allowed[None, None], jnp.exp(scores), 0.0)

    cached = [forward_block((allowed_sets[index], blocks[index][0])) for index in range(reach + 1)]
    denominator = jnp.sum(cached[0], axis=-1, keepdims=True)
    for weight in cached[1:]:
        denominator = denominator + jnp.sum(weight, axis=-1, keepdims=True)
    weights_bf = [(weight / denominator).astype(jnp.bfloat16) for weight in cached]
    attend_zero = jnp.zeros((tokens, kv_heads, group_size, HD), jnp.float32)
    attended = attend_zero
    for index in range(reach + 1):
        attend_prob = weights_bf[index]
        attend_value_block = blocks[index][1]
        attended = attended + jnp.einsum(
            "kgtu,ukd->tkgd", attend_prob, attend_value_block, preferred_element_type=jnp.float32
        )
    row_term = jnp.transpose(jnp.sum(grads_in.astype(jnp.float32) * attended, axis=-1), (1, 2, 0))[
        ..., None
    ]
    dquery_n = attend_zero
    pieces = []
    for index in range(reach + 1):
        prob = weights_bf[index]
        backward_key_block = blocks[index][0]
        value_block = blocks[index][1]
        products = jnp.einsum(
            "tkgd,ukd->kgtu", grads_in, value_block, preferred_element_type=jnp.float32
        )
        dscore = (prob.astype(jnp.float32) * (products - row_term)).astype(jnp.bfloat16)
        dquery_part = jnp.einsum(
            "kgtu,ukd->tkgd", dscore, backward_key_block, preferred_element_type=jnp.float32
        )
        dkey_part = jnp.einsum(
            "kgtu,tkgd->ukd", dscore, query_n, preferred_element_type=jnp.float32
        )
        dvalue_part = jnp.einsum(
            "kgtu,tkgd->ukd", prob, grads_in, preferred_element_type=jnp.float32
        )
        dquery_n = dquery_n + dquery_part
        pieces.append((dkey_part, dvalue_part))
    key_term = jnp.sum(pieces[0][0] * block_hats[0], axis=(0, 1))
    for distance in range(1, reach + 1):
        key_term = key_term + jnp.sum(pieces[distance][0] * block_hats[distance], axis=(0, 1))
    partial_sums = jnp.stack([jnp.sum(dquery_n * query_hat, axis=(0, 1, 2)) * factor, key_term])
    returns = [
        passed_along(
            jnp.concatenate(pieces[distance], axis=-1).astype(jnp.bfloat16), "ctx", -distance
        )
        for distance in range(1, reach + 1)
    ]
    summed = first_rounds(partial_sums)
    summed, *returns = lax.optimization_barrier((summed, *returns))
    dkey_n = pieces[0][0]
    dvalue_sum = pieces[0][1]
    for returned in returns:
        dkey_n = dkey_n + returned[..., :HD].astype(jnp.float32)
        dvalue_sum = dvalue_sum + returned[..., HD:].astype(jnp.float32)
    query_grad = (
        norm_backward(dquery_n, query_hat, query_inv, query_gain, factor)
        .astype(jnp.bfloat16)
        .reshape(1, tokens, -1)
    )
    key_grad = (
        norm_backward(dkey_n, key_hat, key_inv, key_gain, 1.0)
        .astype(jnp.bfloat16)
        .reshape(1, tokens, -1)
    )
    value_grad = dvalue_sum.astype(jnp.bfloat16).reshape(1, tokens, -1)
    summed = middle_rounds(summed)
    summed, query_grad, key_grad, value_grad = lax.optimization_barrier(
        (summed, query_grad, key_grad, value_grad)
    )
    summed = last_round(summed)
    counted = lax.axis_size("dp") * lax.axis_size("ctx") * tokens
    normalizers = jnp.array([[(counted * HQ) ** (-0.5)], [(counted * HK) ** (-0.5)]], jnp.float32)
    return (query_grad, key_grad, value_grad, summed * normalizers)


def solution(mesh):
    in_specs = (
        P("dp", "ctx", "fsdp"),
        P("dp", "ctx", "fsdp"),
        P("dp", "ctx", "fsdp"),
        P("dp", "ctx", "fsdp"),
        P(),
        P(),
        P("dp", "ctx"),
    )
    out_specs = (P("dp", "ctx", "fsdp"), P("dp", "ctx", "fsdp"), P("dp", "ctx", "fsdp"), P())
    return jax.shard_map(shards, mesh=mesh, in_specs=in_specs, out_specs=out_specs, check_vma=False)
```

```python
import jax
import jax.numpy as jnp
from jax import lax
from jax.sharding import PartitionSpec as P

HD = 128
HQ = 16
HK = 8
WINDOW = 1024
QSCALAR = 168


epsilon = 1e-06


def passed_along(value, axis, steps):
    count = lax.axis_size(axis)
    initial, last = (max(0, -steps), min(count, count - steps))
    return lax.ppermute(value, axis, [(source, source + steps) for source in range(initial, last)])


def exchanged_sum(value, axis, stride):
    count = lax.axis_size(axis)
    return value + lax.ppermute(value, axis, [(source, source ^ stride) for source in range(count)])


def three_way_sum(value, axis, stride):
    count = lax.axis_size(axis)
    digit = (lax.axis_index(axis) // stride) % 3
    received = [value]
    for shift in (1, 2):
        pairs = []
        for source in range(count):
            place = (source // stride) % 3
            pairs.append((source, source + ((place + shift) % 3 - place) * stride))
        received.append(lax.ppermute(value, axis, pairs))
    ordered = []
    for place in range(3):
        pick = received[0]
        for shift in (1, 2):
            pick = jnp.where((digit - shift) % 3 == place, received[shift], pick)
        pick = jnp.where(digit == place, received[0], pick)
        ordered.append(pick)
    return ordered[0] + ordered[1] + ordered[2]


def first_rounds(value):
    value = exchanged_sum(value, "fsdp", 1)
    value = exchanged_sum(value, "fsdp", 2)
    value = exchanged_sum(value, "dp", 1)
    value = three_way_sum(value, "ctx", 16)
    count = lax.axis_size("ctx")
    half = count // 2
    return value + lax.ppermute(value, "ctx", [(source, (source + half) % count) for source in range(count)])


def middle_rounds(value):
    for stride in (1, 2, 4):
        value = exchanged_sum(value, "ctx", stride)
    return value


def last_round(value):
    return exchanged_sum(value, "ctx", 8)


def normalize(raw, gain, factor):
    values = raw.astype(jnp.float32)
    inverse = lax.rsqrt(jnp.mean(values * values, axis=-1, keepdims=True) + epsilon)
    unit_rows = values * inverse
    return (unit_rows, inverse, (unit_rows * gain * factor).astype(jnp.bfloat16))


def norm_backward(grad_n, unit_rows, inverse, gain, factor):
    grad_hat = grad_n * gain * factor
    return (grad_hat - unit_rows * jnp.mean(grad_hat * unit_rows, axis=-1, keepdims=True)) * inverse


def shards(query, key, value, out_grad, query_gain, key_gain, list_start):
    tokens = query.shape[1]
    kv_heads = key.shape[2] // HD
    group_size = query.shape[2] // key.shape[2]
    factor = QSCALAR ** (-0.5)
    reach = WINDOW // tokens
    query_hat, query_inv, query_n = normalize(
        query[0].reshape(tokens, kv_heads, group_size, HD), query_gain, factor
    )
    key_raw = key[0].reshape(tokens, kv_heads, HD)
    key_hat, key_inv, key_n = normalize(key_raw, key_gain, 1.0)
    own_values = value[0].reshape(tokens, kv_heads, HD)
    grads_in = out_grad[0].reshape(tokens, kv_heads, group_size, HD)
    starts = list_start[0]
    anchor = lax.axis_index("ctx") * tokens
    query_place = anchor + jnp.arange(tokens, dtype=jnp.int32)
    packed = jnp.concatenate([key_raw, own_values], axis=-1)
    blocks = [(key_n, own_values)]
    block_hats = [key_hat]
    for distance in range(1, reach + 1):
        arrived = passed_along(packed, "ctx", distance)
        arrived_hat, _, arrived_n = normalize(arrived[..., :HD], key_gain, 1.0)
        blocks.append((arrived_n, arrived[..., HD:]))
        block_hats.append(arrived_hat)
    allowed_sets = []
    for distance in range(reach + 1):
        key_place = anchor - distance * tokens + jnp.arange(tokens, dtype=jnp.int32)
        allowed_sets.append(
            (key_place[None, :] >= starts[:, None])
            & (key_place[None, :] <= query_place[:, None])
            & (query_place[:, None] - key_place[None, :] < WINDOW)
        )

    def forward_block(operands):
        allowed, key_block = operands
        scores = jnp.einsum(
            "tkgd,ukd->kgtu", query_n, key_block, preferred_element_type=jnp.float32
        )
        return jnp.where(allowed[None, None], jnp.exp(scores), 0.0)

    cached = [forward_block((allowed_sets[index], blocks[index][0])) for index in range(reach + 1)]
    denominator = jnp.sum(cached[0], axis=-1, keepdims=True)
    for weight in cached[1:]:
        denominator = denominator + jnp.sum(weight, axis=-1, keepdims=True)
    weights_bf = [(weight / denominator).astype(jnp.bfloat16) for weight in cached]
    attend_zero = jnp.zeros((tokens, kv_heads, group_size, HD), jnp.float32)
    attended = attend_zero
    for index in range(reach + 1):
        attend_prob = weights_bf[index]
        attend_value_block = blocks[index][1]
        attended = attended + jnp.einsum(
            "kgtu,ukd->tkgd", attend_prob, attend_value_block, preferred_element_type=jnp.float32
        )
    row_term = jnp.transpose(jnp.sum(grads_in.astype(jnp.float32) * attended, axis=-1), (1, 2, 0))[
        ..., None
    ]
    dquery_n = attend_zero
    pieces = []
    for index in range(reach + 1):
        prob = weights_bf[index]
        backward_key_block = blocks[index][0]
        value_block = blocks[index][1]
        products = jnp.einsum(
            "tkgd,ukd->kgtu", grads_in, value_block, preferred_element_type=jnp.float32
        )
        dscore = (prob.astype(jnp.float32) * (products - row_term)).astype(jnp.bfloat16)
        dquery_part = jnp.einsum(
            "kgtu,ukd->tkgd", dscore, backward_key_block, preferred_element_type=jnp.float32
        )
        dkey_part = jnp.einsum(
            "kgtu,tkgd->ukd", dscore, query_n, preferred_element_type=jnp.float32
        )
        dvalue_part = jnp.einsum(
            "kgtu,tkgd->ukd", prob, grads_in, preferred_element_type=jnp.float32
        )
        dquery_n = dquery_n + dquery_part
        pieces.append((dkey_part, dvalue_part))
    key_term = jnp.sum(pieces[0][0] * block_hats[0], axis=(0, 1))
    for distance in range(1, reach + 1):
        key_term = key_term + jnp.sum(pieces[distance][0] * block_hats[distance], axis=(0, 1))
    partial_sums = jnp.stack([jnp.sum(dquery_n * query_hat, axis=(0, 1, 2)) * factor, key_term])
    returns = [
        passed_along(
            jnp.concatenate(pieces[distance], axis=-1).astype(jnp.bfloat16), "ctx", -distance
        )
        for distance in range(1, reach + 1)
    ]
    summed = first_rounds(partial_sums)
    summed, *returns = lax.optimization_barrier((summed, *returns))
    dkey_n = pieces[0][0]
    dvalue_sum = pieces[0][1]
    for returned in returns:
        dkey_n = dkey_n + returned[..., :HD].astype(jnp.float32)
        dvalue_sum = dvalue_sum + returned[..., HD:].astype(jnp.float32)
    query_grad = (
        norm_backward(dquery_n, query_hat, query_inv, query_gain, factor)
        .astype(jnp.bfloat16)
        .reshape(1, tokens, -1)
    )
    key_grad = (
        norm_backward(dkey_n, key_hat, key_inv, key_gain, 1.0)
        .astype(jnp.bfloat16)
        .reshape(1, tokens, -1)
    )
    value_grad = dvalue_sum.astype(jnp.bfloat16).reshape(1, tokens, -1)
    summed = middle_rounds(summed)
    summed, query_grad, key_grad, value_grad = lax.optimization_barrier(
        (summed, query_grad, key_grad, value_grad)
    )
    summed = last_round(summed)
    counted = lax.axis_size("dp") * lax.axis_size("ctx") * tokens
    normalizers = jnp.array([[(counted * HQ) ** (-0.5)], [(counted * HK) ** (-0.5)]], jnp.float32)
    return (query_grad, key_grad, value_grad, summed * normalizers)


def solution(mesh):
    in_specs = (
        P("dp", "ctx", "fsdp"),
        P("dp", "ctx", "fsdp"),
        P("dp", "ctx", "fsdp"),
        P("dp", "ctx", "fsdp"),
        P(),
        P(),
        P("dp", "ctx"),
    )
    out_specs = (P("dp", "ctx", "fsdp"), P("dp", "ctx", "fsdp"), P("dp", "ctx", "fsdp"), P())
    return jax.shard_map(shards, mesh=mesh, in_specs=in_specs, out_specs=out_specs, check_vma=False)
```

```python
import jax
import jax.numpy as jnp
from jax import lax
from jax.sharding import PartitionSpec as P

HD = 128
HQ = 16
HK = 8
WINDOW = 1024
QSCALAR = 168


epsilon = 1e-06


def passed_along(value, axis, steps):
    count = lax.axis_size(axis)
    initial, last = (max(0, -steps), min(count, count - steps))
    return lax.ppermute(value, axis, [(source, source + steps) for source in range(initial, last)])


def exchanged_sum(value, axis, stride):
    count = lax.axis_size(axis)
    return value + lax.ppermute(value, axis, [(source, source ^ stride) for source in range(count)])


def three_way_sum(value, axis, stride):
    count = lax.axis_size(axis)
    digit = (lax.axis_index(axis) // stride) % 3
    received = [value]
    for shift in (1, 2):
        pairs = []
        for source in range(count):
            place = (source // stride) % 3
            pairs.append((source, source + ((place + shift) % 3 - place) * stride))
        received.append(lax.ppermute(value, axis, pairs))
    ordered = []
    for place in range(3):
        pick = received[0]
        for shift in (1, 2):
            pick = jnp.where((digit - shift) % 3 == place, received[shift], pick)
        pick = jnp.where(digit == place, received[0], pick)
        ordered.append(pick)
    return ordered[0] + ordered[1] + ordered[2]


def first_rounds(value):
    value = exchanged_sum(value, "fsdp", 1)
    value = exchanged_sum(value, "fsdp", 2)
    value = exchanged_sum(value, "dp", 1)
    value = three_way_sum(value, "ctx", 16)
    count = lax.axis_size("ctx")
    half = count // 2
    return value + lax.ppermute(value, "ctx", [(source, (source + half) % count) for source in range(count)])


def middle_rounds(value):
    return exchanged_sum(value, "ctx", 1)


def last_round(value):
    for stride in (2, 4, 8):
        value = exchanged_sum(value, "ctx", stride)
    return value


def normalize(raw, gain, factor):
    values = raw.astype(jnp.float32)
    inverse = lax.rsqrt(jnp.mean(values * values, axis=-1, keepdims=True) + epsilon)
    unit_rows = values * inverse
    return (unit_rows, inverse, (unit_rows * gain * factor).astype(jnp.bfloat16))


def norm_backward(grad_n, unit_rows, inverse, gain, factor):
    grad_hat = grad_n * gain * factor
    return (grad_hat - unit_rows * jnp.mean(grad_hat * unit_rows, axis=-1, keepdims=True)) * inverse


def shards(query, key, value, out_grad, query_gain, key_gain, list_start):
    tokens = query.shape[1]
    kv_heads = key.shape[2] // HD
    group_size = query.shape[2] // key.shape[2]
    factor = QSCALAR ** (-0.5)
    reach = WINDOW // tokens
    query_hat, query_inv, query_n = normalize(
        query[0].reshape(tokens, kv_heads, group_size, HD), query_gain, factor
    )
    key_raw = key[0].reshape(tokens, kv_heads, HD)
    key_hat, key_inv, key_n = normalize(key_raw, key_gain, 1.0)
    own_values = value[0].reshape(tokens, kv_heads, HD)
    grads_in = out_grad[0].reshape(tokens, kv_heads, group_size, HD)
    starts = list_start[0]
    anchor = lax.axis_index("ctx") * tokens
    query_place = anchor + jnp.arange(tokens, dtype=jnp.int32)
    packed = jnp.concatenate([key_raw, own_values], axis=-1)
    blocks = [(key_n, own_values)]
    block_hats = [key_hat]
    for distance in range(1, reach + 1):
        arrived = passed_along(packed, "ctx", distance)
        arrived_hat, _, arrived_n = normalize(arrived[..., :HD], key_gain, 1.0)
        blocks.append((arrived_n, arrived[..., HD:]))
        block_hats.append(arrived_hat)
    allowed_sets = []
    for distance in range(reach + 1):
        key_place = anchor - distance * tokens + jnp.arange(tokens, dtype=jnp.int32)
        allowed_sets.append(
            (key_place[None, :] >= starts[:, None])
            & (key_place[None, :] <= query_place[:, None])
            & (query_place[:, None] - key_place[None, :] < WINDOW)
        )

    def forward_block(operands):
        allowed, key_block = operands
        scores = jnp.einsum(
            "tkgd,ukd->kgtu", query_n, key_block, preferred_element_type=jnp.float32
        )
        return jnp.where(allowed[None, None], jnp.exp(scores), 0.0)

    cached = [forward_block((allowed_sets[index], blocks[index][0])) for index in range(reach + 1)]
    denominator = jnp.sum(cached[0], axis=-1, keepdims=True)
    for weight in cached[1:]:
        denominator = denominator + jnp.sum(weight, axis=-1, keepdims=True)
    weights_bf = [(weight / denominator).astype(jnp.bfloat16) for weight in cached]
    attend_zero = jnp.zeros((tokens, kv_heads, group_size, HD), jnp.float32)
    attended = attend_zero
    for index in range(reach + 1):
        attend_prob = weights_bf[index]
        attend_value_block = blocks[index][1]
        attended = attended + jnp.einsum(
            "kgtu,ukd->tkgd", attend_prob, attend_value_block, preferred_element_type=jnp.float32
        )
    row_term = jnp.transpose(jnp.sum(grads_in.astype(jnp.float32) * attended, axis=-1), (1, 2, 0))[
        ..., None
    ]
    dquery_n = attend_zero
    pieces = []
    for index in range(reach + 1):
        prob = weights_bf[index]
        backward_key_block = blocks[index][0]
        value_block = blocks[index][1]
        products = jnp.einsum(
            "tkgd,ukd->kgtu", grads_in, value_block, preferred_element_type=jnp.float32
        )
        dscore = (prob.astype(jnp.float32) * (products - row_term)).astype(jnp.bfloat16)
        dquery_part = jnp.einsum(
            "kgtu,ukd->tkgd", dscore, backward_key_block, preferred_element_type=jnp.float32
        )
        dkey_part = jnp.einsum(
            "kgtu,tkgd->ukd", dscore, query_n, preferred_element_type=jnp.float32
        )
        dvalue_part = jnp.einsum(
            "kgtu,tkgd->ukd", prob, grads_in, preferred_element_type=jnp.float32
        )
        dquery_n = dquery_n + dquery_part
        pieces.append((dkey_part, dvalue_part))
    key_term = jnp.sum(pieces[0][0] * block_hats[0], axis=(0, 1))
    for distance in range(1, reach + 1):
        key_term = key_term + jnp.sum(pieces[distance][0] * block_hats[distance], axis=(0, 1))
    partial_sums = jnp.stack([jnp.sum(dquery_n * query_hat, axis=(0, 1, 2)) * factor, key_term])
    returns = [
        passed_along(
            jnp.concatenate(pieces[distance], axis=-1).astype(jnp.bfloat16), "ctx", -distance
        )
        for distance in range(1, reach + 1)
    ]
    summed = first_rounds(partial_sums)
    summed, *returns = lax.optimization_barrier((summed, *returns))
    dkey_n = pieces[0][0]
    dvalue_sum = pieces[0][1]
    for returned in returns:
        dkey_n = dkey_n + returned[..., :HD].astype(jnp.float32)
        dvalue_sum = dvalue_sum + returned[..., HD:].astype(jnp.float32)
    query_grad = (
        norm_backward(dquery_n, query_hat, query_inv, query_gain, factor)
        .astype(jnp.bfloat16)
        .reshape(1, tokens, -1)
    )
    key_grad = (
        norm_backward(dkey_n, key_hat, key_inv, key_gain, 1.0)
        .astype(jnp.bfloat16)
        .reshape(1, tokens, -1)
    )
    value_grad = dvalue_sum.astype(jnp.bfloat16).reshape(1, tokens, -1)
    summed = middle_rounds(summed)
    summed, query_grad, key_grad, value_grad = lax.optimization_barrier(
        (summed, query_grad, key_grad, value_grad)
    )
    summed = last_round(summed)
    counted = lax.axis_size("dp") * lax.axis_size("ctx") * tokens
    normalizers = jnp.array([[(counted * HQ) ** (-0.5)], [(counted * HK) ** (-0.5)]], jnp.float32)
    return (query_grad, key_grad, value_grad, summed * normalizers)


def solution(mesh):
    in_specs = (
        P("dp", "ctx", "fsdp"),
        P("dp", "ctx", "fsdp"),
        P("dp", "ctx", "fsdp"),
        P("dp", "ctx", "fsdp"),
        P(),
        P(),
        P("dp", "ctx"),
    )
    out_specs = (P("dp", "ctx", "fsdp"), P("dp", "ctx", "fsdp"), P("dp", "ctx", "fsdp"), P())
    return jax.shard_map(shards, mesh=mesh, in_specs=in_specs, out_specs=out_specs, check_vma=False)
```
